256 devices in a mesh: dp: 8 (over y_lo, x), space: 32 (over y_hi, z, core).
Axes of the slice: x: 4, y: 4 (y_hi: 2, y_lo: 2; y = y_hi * 2 + y_lo), z: 8, core: 2. Of those that a mesh axis runs over, the one named last changes fastest.
Arguments:
- images: bfloat16 [8, 256, 64, 1536], P('dp', 'space'), may hold values from -8 to 8
- dw_kernel: bfloat16 [7, 7, 1536], replicated, may hold values from -0.875 to 0.875
- dw_bias: float32 [1536], replicated, may hold values from -3 to 3
- ln_gain: float32 [1536], replicated, may hold values from 0.1 to 1.9
- ln_shift: float32 [1536], replicated, may hold values from -2 to 2
- proj: bfloat16 [1536, 1024], replicated, may hold values from -0.15625 to 0.15625
- text: float32 [8, 1024], P('dp'), may hold values from -6 to 6
- logit_scale: float32 [1], replicated, may hold values from 10 to 100
Outputs:
- loss: float32 [], replicated
- grad_images: bfloat16 [8, 256, 64, 1536], P('dp', 'space')
- kernel_grad: float32 [7, 7, 1536], replicated
- text_grad: float32 [8, 1024], P('dp')
The draws below stay inside these ranges and needn't reach their ends.
All inputs are finite; a program needn't handle non-finite values.
Results may differ from the reference program's by a relative error of at most 0.0013.
Values may be sent and summed in bfloat16 or wider, within the bound.
No kernel may reach another device: no remote copies, remote signals or barrier semaphores. Data moves between devices by JAX's collectives and lax.ppermute only.
A program may use at most 128 MiB of HBM per device.

```python
import jax
import jax.numpy as jnp
from jax import lax

CHANNELS = 1536
EMBED = 1024
KERNEL = 7
WIDTH = 64
BATCH = 8
HEIGHT = 256


def draw_images(key, part):
    first, second, third = jax.random.split(key, 3)
    offsets = jax.random.normal(first, (BATCH, 1, 1, CHANNELS), jnp.float32)
    channel_scale = jnp.exp(jax.random.uniform(third, (1, 1, 1, CHANNELS), jnp.float32, -1.2, 1.2))
    noise = jax.random.normal(second, (BATCH, HEIGHT, WIDTH, CHANNELS), jnp.float32)
    row_amp = 1.0 + 2.0 * jnp.arange(HEIGHT, dtype=jnp.float32) / HEIGHT
    image_amp = 1.0 + 2.0 * jnp.arange(BATCH, dtype=jnp.float32) / BATCH
    amplitude = row_amp[None, :, None, None] * image_amp[:, None, None, None]
    values = amplitude * (0.8 * offsets + 0.5 * noise * channel_scale)
    return jnp.clip(values, -8.0, 8.0).astype(jnp.bfloat16)


def draw_logit_scale(key, part):
    return jax.random.uniform(key, (1,), jnp.float32, 10.0, 30.0)


def level_of(rng, shape, shards, smallest, top_value):
    def one(dim, shards_of):
        heights = jax.random.uniform(jax.random.fold_in(jax.random.fold_in(rng, 6), dim), (shards_of,), jnp.float32, smallest / len(shards), top_value / len(shards))
        return jnp.repeat(jnp.exp(heights), shape[dim] // shards_of).reshape((-1,) + (1,) * (len(shape) - dim - 1))

    level = one(*shards[0])
    for cut in shards[1:]:
        level = level * one(*cut)
    return level


def scatter_about(key, extent, width, limit, shards=(), held_as=jnp.bfloat16):
    values = width * jax.random.normal(key, extent, jnp.float32)
    if shards:
        values = values * level_of(key, extent, shards, -0.22, 0.18)
    return jnp.clip(values, -limit, limit).astype(held_as)


def setup_inputs(seed: int = 0) -> dict:
    key_of = jax.random.split(jax.random.key(seed), 9)
    return {
        "images": draw_images(jax.random.fold_in(key_of[8], 71), 0),
        "dw_kernel": scatter_about(key_of[1], (KERNEL, KERNEL, CHANNELS), (KERNEL * KERNEL) ** -0.5, 0.875),
        "dw_bias": scatter_about(key_of[2], (CHANNELS,), 0.5, 3.0, (), jnp.float32),
        "ln_gain": jnp.clip(1.0 + 0.18 * jax.random.normal(key_of[3], (CHANNELS,), jnp.float32), 0.1, 1.9),
        "ln_shift": scatter_about(key_of[4], (CHANNELS,), 0.3, 2.0, (), jnp.float32),
        "proj": scatter_about(key_of[5], (CHANNELS, EMBED), CHANNELS ** -0.5, 0.15625),
        "text": scatter_about(key_of[6], (BATCH, EMBED), 1.0, 6.0, ((0, 8),), jnp.float32),
        "logit_scale": draw_logit_scale(jax.random.fold_in(key_of[8], 71), 0),
    }


def normalize(values):
    centre_value = lax.optimization_barrier(jnp.mean(values, axis=-1, keepdims=True))
    centred = values - centre_value
    spread = lax.optimization_barrier(jnp.mean(centred * centred, axis=-1, keepdims=True))
    inv_dev = lax.rsqrt(spread + 1e-06)
    return (centred * inv_dev, inv_dev)

def convolve(padded, kernel_float, row_count, col_count):
    result = jnp.zeros((row_count, col_count, padded.shape[-1]), jnp.float32)
    for a in range(kernel_float.shape[0]):
        for d in range(kernel_float.shape[1]):
            result = result + padded[a:a + row_count, d:d + col_count, :] * kernel_float[a, d]
    return result

def logsum(scores, axis):
    highest = lax.optimization_barrier(jnp.max(scores, axis=axis, keepdims=True))
    return jnp.squeeze(highest, axis) + jnp.log(lax.optimization_barrier(jnp.sum(jnp.exp(scores - highest), axis=axis)))

def reference(images, dw_kernel, dw_bias, ln_gain, ln_shift, proj, text, logit_scale):
    reach_rows = KERNEL // 2
    kernel_float = dw_kernel.astype(jnp.float32)
    row_count = images.shape[1]
    col_count = images.shape[2]
    pixel_count = row_count * col_count

    def forward_one(single_image):
        padded = jnp.pad(single_image.astype(jnp.float32), ((reach_rows, reach_rows), (reach_rows, reach_rows), (0, 0)))
        conv_out = convolve(padded, kernel_float, row_count, col_count) + dw_bias
        normed, inv_dev = normalize(conv_out)
        return lax.optimization_barrier(jnp.sum(normed * ln_gain + ln_shift, axis=(0, 1))) / pixel_count
    pooled = lax.map(forward_one, images)
    proj_float = proj.astype(jnp.float32)
    embedded = jnp.dot(pooled, proj_float, precision=lax.Precision.HIGHEST)
    emb_norm = jnp.sqrt(lax.optimization_barrier(jnp.sum(embedded * embedded, axis=-1, keepdims=True)))
    unit_img = embedded / emb_norm
    text_norm = jnp.sqrt(lax.optimization_barrier(jnp.sum(text * text, axis=-1, keepdims=True)))
    unit_txt = text / text_norm
    factor = logit_scale[0]
    scores = factor * jnp.dot(unit_img, unit_txt.T, precision=lax.Precision.HIGHEST)
    row_logsum = logsum(scores, 1)
    col_logsum = logsum(scores, 0)
    diagonal = jnp.diagonal(scores)
    batch_count = scores.shape[0]
    loss = (jnp.sum(row_logsum - diagonal) + jnp.sum(col_logsum - diagonal)) / (2 * batch_count)
    identity = jnp.eye(batch_count, dtype=jnp.float32)
    score_grad = 0.5 * (jnp.exp(scores - row_logsum[:, None]) + jnp.exp(scores - col_logsum[None, :])) - identity
    unit_img_grad = factor * jnp.dot(score_grad, unit_txt, precision=lax.Precision.HIGHEST)
    unit_txt_grad = factor * jnp.dot(score_grad.T, unit_img, precision=lax.Precision.HIGHEST)
    text_grad = (unit_txt_grad - unit_txt * lax.optimization_barrier(jnp.sum(unit_txt * unit_txt_grad, axis=-1, keepdims=True))) / text_norm
    emb_grad = (unit_img_grad - unit_img * lax.optimization_barrier(jnp.sum(unit_img * unit_img_grad, axis=-1, keepdims=True))) / emb_norm
    weighted = jnp.dot(emb_grad, proj_float.T, precision=lax.Precision.HIGHEST) * ln_gain

    def backward_one(inputs):
        single_image, weight_row = inputs
        padded = jnp.pad(single_image.astype(jnp.float32), ((reach_rows, reach_rows), (reach_rows, reach_rows), (0, 0)))
        conv_out = convolve(padded, kernel_float, row_count, col_count) + dw_bias
        normed, inv_dev = normalize(conv_out)
        weight_mean = jnp.mean(weight_row)
        spread_term = lax.optimization_barrier(jnp.mean(weight_row * normed, axis=-1, keepdims=True))
        pixel_grad = inv_dev * (weight_row - weight_mean - normed * spread_term)
        grad_pad = jnp.pad(pixel_grad, ((reach_rows, reach_rows), (reach_rows, reach_rows), (0, 0)))
        input_grad = jnp.zeros_like(pixel_grad)
        for a in range(KERNEL):
            for d in range(KERNEL):
                start_row = 2 * reach_rows - a
                start_col = 2 * reach_rows - d
                input_grad = input_grad + kernel_float[a, d] * grad_pad[start_row:start_row + row_count, start_col:start_col + col_count, :]
        kernel_terms = jnp.stack([jnp.stack([lax.optimization_barrier(jnp.sum(pixel_grad * padded[a:a + row_count, d:d + col_count, :], axis=(0, 1))) for d in range(KERNEL)]) for a in range(KERNEL)])
        return (input_grad.astype(jnp.bfloat16), kernel_terms)
    grad_images, kernel_terms = lax.map(backward_one, (images, weighted))
    kernel_grad = lax.optimization_barrier(jnp.sum(kernel_terms, axis=0)) / pixel_count
    return (loss, grad_images, kernel_grad, text_grad)
```

```python
import jax
import jax.numpy as jnp
from jax import lax
from jax.sharding import PartitionSpec as P


def with_halo(block, sides, width):
    for axis, dim in sides:
        count = lax.axis_size(axis)
        forward = [(i, i + 1) for i in range(count - 1)]
        backward = [(target, source) for source, target in forward]
        low = lax.ppermute(
            lax.slice_in_dim(block, block.shape[dim] - width, None, axis=dim), axis, forward
        )
        high = lax.ppermute(lax.slice_in_dim(block, 0, width, axis=dim), axis, backward)
        block = jnp.concatenate([low, block, high], axis=dim)
    return block


def butterfly_sum(values, axes):
    for axis in axes:
        count = lax.axis_size(axis)
        if count & (count - 1):
            values = lax.psum(values, axis)
            continue
        step = 1
        while step < count:
            pairs = [(i, i ^ step) for i in range(count)]
            values = values + lax.ppermute(values, axis, pairs)
            step *= 2
    return values


def normalize(values):
    centre_value = jnp.mean(values, axis=-1, keepdims=True)
    centred = values - centre_value
    spread = jnp.mean(centred * centred, axis=-1, keepdims=True)
    inv_dev = lax.rsqrt(spread + 1e-06)
    return (centred * inv_dev, inv_dev)


def convolve(padded, kernel_float, row_count, col_count):
    result = None
    for a in range(kernel_float.shape[0]):
        for d in range(kernel_float.shape[1]):
            product = padded[:, a : a + row_count, d : d + col_count, :] * kernel_float[a, d]
            result = product if result is None else result + product
    return result


def logsum(scores, axis):
    highest = jnp.max(scores, axis=axis, keepdims=True)
    return jnp.squeeze(highest, axis) + jnp.log(jnp.sum(jnp.exp(scores - highest), axis=axis))


def shards(images, dw_kernel, dw_bias, ln_gain, ln_shift, proj, text, logit_scale):
    batch_dev, row_count, col_count, channels = images.shape
    height = row_count * lax.axis_size("space")
    pixel_count = height * col_count
    batch_count = batch_dev * lax.axis_size("dp")
    reach_rows = dw_kernel.shape[0] // 2
    kernel_float = dw_kernel.astype(jnp.float32)
    extended = with_halo(images, (("space", 1),), reach_rows)
    padded_all = jnp.pad(
        extended.astype(jnp.float32), ((0, 0), (0, 0), (reach_rows, reach_rows), (0, 0))
    )
    conv_out = convolve(padded_all, kernel_float, row_count, col_count) + dw_bias
    normed, inv_dev = normalize(conv_out)
    pool_part = jnp.sum(normed * ln_gain + ln_shift, axis=(1, 2))
    pool_sum = butterfly_sum(pool_part, ("space",))
    first_row = lax.axis_index("dp") * batch_dev
    packed = jnp.concatenate([pool_sum, text], axis=1)
    table = lax.dynamic_update_slice(
        jnp.zeros((batch_count, packed.shape[1]), jnp.float32), packed, (first_row, 0)
    )
    table = butterfly_sum(table, ("dp",))
    pooled = table[:, :channels] / pixel_count
    all_text = table[:, channels:]
    proj_float = proj.astype(jnp.float32)
    embedded = jnp.dot(pooled, proj_float, precision=lax.Precision.HIGHEST)
    emb_norm = jnp.sqrt(jnp.sum(embedded * embedded, axis=-1, keepdims=True))
    unit_img = embedded / emb_norm
    text_norm = jnp.sqrt(jnp.sum(all_text * all_text, axis=-1, keepdims=True))
    unit_txt = all_text / text_norm
    factor = logit_scale[0]
    scores = factor * jnp.dot(unit_img, unit_txt.T, precision=lax.Precision.HIGHEST)
    row_logsum = logsum(scores, 1)
    col_logsum = logsum(scores, 0)
    identity = jnp.eye(batch_count, dtype=jnp.float32)
    diagonal = jnp.sum(scores * identity, axis=1)
    loss = (jnp.sum(row_logsum - diagonal) + jnp.sum(col_logsum - diagonal)) / (2 * batch_count)
    score_grad = (
        0.5
        * (
            jnp.exp(scores - row_logsum[:, None])
            + jnp.exp(scores - col_logsum[None, :])
        )
        - identity
    )
    unit_img_grad = factor * jnp.dot(score_grad, unit_txt, precision=lax.Precision.HIGHEST)
    unit_txt_grad = factor * jnp.dot(score_grad.T, unit_img, precision=lax.Precision.HIGHEST)
    text_grad_all = (
        unit_txt_grad - unit_txt * jnp.sum(unit_txt * unit_txt_grad, axis=-1, keepdims=True)
    ) / text_norm
    emb_grad_all = (
        unit_img_grad - unit_img * jnp.sum(unit_img * unit_img_grad, axis=-1, keepdims=True)
    ) / emb_norm
    text_grad = lax.dynamic_slice_in_dim(text_grad_all, first_row, batch_dev, axis=0)
    emb_grad = lax.dynamic_slice_in_dim(emb_grad_all, first_row, batch_dev, axis=0)
    weighted = jnp.dot(emb_grad, proj_float.T, precision=lax.Precision.HIGHEST) * ln_gain
    weight_rows = weighted[:, None, None, :]
    weight_mean = jnp.mean(weighted, axis=-1)[:, None, None, None]
    spread_term = jnp.mean(weight_rows * normed, axis=-1, keepdims=True)
    grad_own = inv_dev * (weight_rows - weight_mean - normed * spread_term)
    grad_wide = with_halo(grad_own, (("space", 1),), reach_rows)
    grad_pad = jnp.pad(grad_wide, ((0, 0), (0, 0), (reach_rows, reach_rows), (0, 0)))
    input_grad = None
    for a in range(kernel_float.shape[0]):
        for d in range(kernel_float.shape[1]):
            start_row = 2 * reach_rows - a
            start_col = 2 * reach_rows - d
            product = (
                kernel_float[a, d]
                * grad_pad[
                    :, start_row : start_row + row_count, start_col : start_col + col_count, :
                ]
            )
            input_grad = product if input_grad is None else input_grad + product
    kernel_part = jnp.stack(
        [
            jnp.stack(
                [
                    jnp.sum(
                        grad_own * padded_all[:, a : a + row_count, d : d + col_count, :],
                        axis=(0, 1, 2),
                    )
                    for d in range(kernel_float.shape[1])
                ]
            )
            for a in range(kernel_float.shape[0])
        ]
    )
    kernel_grad = butterfly_sum(kernel_part, ("space", "dp")) / pixel_count
    return (loss, input_grad.astype(jnp.bfloat16), kernel_grad, text_grad)


def solution(mesh):
    placed = (P("dp", "space", None, None), P(), P(), P(), P(), P(), P("dp", None), P())
    return jax.shard_map(
        shards,
        mesh=mesh,
        in_specs=placed,
        out_specs=(P(), P("dp", "space", None, None), P(), P("dp", None)),
        check_vma=False,
    )
```

```python
import jax
import jax.numpy as jnp
from jax import lax
from jax.sharding import PartitionSpec as P


def with_halo(block, sides, width):
    for axis, dim in sides:
        count = lax.axis_size(axis)
        forward = [(i, i + 1) for i in range(count - 1)]
        backward = [(target, source) for source, target in forward]
        low = lax.ppermute(
            lax.slice_in_dim(block, block.shape[dim] - width, None, axis=dim), axis, forward
        )
        high = lax.ppermute(lax.slice_in_dim(block, 0, width, axis=dim), axis, backward)
        block = jnp.concatenate([low, block, high], axis=dim)
    return block


def butterfly_sum(values, axes):
    for axis in axes:
        count = lax.axis_size(axis)
        if count & (count - 1):
            values = lax.psum(values, axis)
            continue
        step = 1
        while step < count:
            pairs = [(i, i ^ step) for i in range(count)]
            values = values + lax.ppermute(values, axis, pairs)
            step *= 2
    return values


def normalize(values):
    centre_value = jnp.mean(values, axis=-1, keepdims=True)
    centred = values - centre_value
    spread = jnp.mean(centred * centred, axis=-1, keepdims=True)
    inv_dev = lax.rsqrt(spread + 1e-06)
    return (centred * inv_dev, inv_dev)


def depthwise(extended, kernel, reach_cols, **options):
    channels = kernel.shape[-1]
    return lax.conv_general_dilated(
        extended,
        kernel.reshape(kernel.shape[0], kernel.shape[1], 1, channels),
        (1, 1),
        ((0, 0), (reach_cols, reach_cols)),
        dimension_numbers=("NHWC", "HWIO", "NHWC"),
        feature_group_count=channels,
        **options,
    )


def logsum(scores, axis):
    highest = jnp.max(scores, axis=axis, keepdims=True)
    return jnp.squeeze(highest, axis) + jnp.log(jnp.sum(jnp.exp(scores - highest), axis=axis))


def shards(images, dw_kernel, dw_bias, ln_gain, ln_shift, proj, text, logit_scale):
    batch_dev, row_count, col_count, channels = images.shape
    height = row_count * lax.axis_size("space")
    pixel_count = height * col_count
    batch_count = batch_dev * lax.axis_size("dp")
    reach_rows = dw_kernel.shape[0] // 2
    kernel_float = dw_kernel.astype(jnp.float32)
    extended = with_halo(images, (("space", 1),), reach_rows)
    padded_all = jnp.pad(
        extended.astype(jnp.float32), ((0, 0), (0, 0), (reach_rows, reach_rows), (0, 0))
    )
    conv_out = (
        depthwise(extended, dw_kernel, reach_rows, preferred_element_type=jnp.float32) + dw_bias
    )
    normed, inv_dev = normalize(conv_out)
    pool_part = jnp.sum(normed * ln_gain + ln_shift, axis=(1, 2))
    pool_sum = butterfly_sum(pool_part, ("space",))
    first_row = lax.axis_index("dp") * batch_dev
    packed = jnp.concatenate([pool_sum, text], axis=1)
    table = lax.dynamic_update_slice(
        jnp.zeros((batch_count, packed.shape[1]), jnp.float32), packed, (first_row, 0)
    )
    table = butterfly_sum(table, ("dp",))
    pooled = table[:, :channels] / pixel_count
    all_text = table[:, channels:]
    proj_float = proj.astype(jnp.float32)
    embedded = jnp.dot(pooled, proj_float, precision=lax.Precision.HIGHEST)
    emb_norm = jnp.sqrt(jnp.sum(embedded * embedded, axis=-1, keepdims=True))
    unit_img = embedded / emb_norm
    text_norm = jnp.sqrt(jnp.sum(all_text * all_text, axis=-1, keepdims=True))
    unit_txt = all_text / text_norm
    factor = logit_scale[0]
    scores = factor * jnp.dot(unit_img, unit_txt.T, precision=lax.Precision.HIGHEST)
    row_logsum = logsum(scores, 1)
    col_logsum = logsum(scores, 0)
    identity = jnp.eye(batch_count, dtype=jnp.float32)
    diagonal = jnp.sum(scores * identity, axis=1)
    loss = (jnp.sum(row_logsum - diagonal) + jnp.sum(col_logsum - diagonal)) / (2 * batch_count)
    score_grad = (
        0.5
        * (
            jnp.exp(scores - row_logsum[:, None])
            + jnp.exp(scores - col_logsum[None, :])
        )
        - identity
    )
    unit_img_grad = factor * jnp.dot(score_grad, unit_txt, precision=lax.Precision.HIGHEST)
    unit_txt_grad = factor * jnp.dot(score_grad.T, unit_img, precision=lax.Precision.HIGHEST)
    text_grad_all = (
        unit_txt_grad - unit_txt * jnp.sum(unit_txt * unit_txt_grad, axis=-1, keepdims=True)
    ) / text_norm
    emb_grad_all = (
        unit_img_grad - unit_img * jnp.sum(unit_img * unit_img_grad, axis=-1, keepdims=True)
    ) / emb_norm
    text_grad = lax.dynamic_slice_in_dim(text_grad_all, first_row, batch_dev, axis=0)
    emb_grad = lax.dynamic_slice_in_dim(emb_grad_all, first_row, batch_dev, axis=0)
    weighted = jnp.dot(emb_grad, proj_float.T, precision=lax.Precision.HIGHEST) * ln_gain
    weight_rows = weighted[:, None, None, :]
    weight_mean = jnp.mean(weighted, axis=-1)[:, None, None, None]
    spread_term = jnp.mean(weight_rows * normed, axis=-1, keepdims=True)
    grad_own = inv_dev * (weight_rows - weight_mean - normed * spread_term)
    grad_wide = with_halo(grad_own, (("space", 1),), reach_rows)
    input_grad = depthwise(
        grad_wide, kernel_float[::-1, ::-1], reach_rows, precision=lax.Precision.HIGHEST
    )
    kernel_part = jnp.stack(
        [
            jnp.stack(
                [
                    jnp.sum(
                        grad_own * padded_all[:, a : a + row_count, d : d + col_count, :],
                        axis=(0, 1, 2),
                    )
                    for d in range(kernel_float.shape[1])
                ]
            )
            for a in range(kernel_float.shape[0])
        ]
    )
    kernel_grad = butterfly_sum(kernel_part, ("space", "dp")) / pixel_count
    return (loss, input_grad.astype(jnp.bfloat16), kernel_grad, text_grad)


def solution(mesh):
    placed = (P("dp", "space", None, None), P(), P(), P(), P(), P(), P("dp", None), P())
    return jax.shard_map(
        shards,
        mesh=mesh,
        in_specs=placed,
        out_specs=(P(), P("dp", "space", None, None), P(), P("dp", None)),
        check_vma=False,
    )
```

```python
import jax
import jax.numpy as jnp
from jax import lax
from jax.experimental import pallas as pl
from jax.sharding import PartitionSpec as P


def with_halo(block, sides, width):
    for axis, dim in sides:
        count = lax.axis_size(axis)
        forward = [(i, i + 1) for i in range(count - 1)]
        backward = [(target, source) for source, target in forward]
        low = lax.ppermute(
            lax.slice_in_dim(block, block.shape[dim] - width, None, axis=dim), axis, forward
        )
        high = lax.ppermute(lax.slice_in_dim(block, 0, width, axis=dim), axis, backward)
        block = jnp.concatenate([low, block, high], axis=dim)
    return block


def butterfly_sum(values, axes):
    for axis in axes:
        count = lax.axis_size(axis)
        if count & (count - 1):
            values = lax.psum(values, axis)
            continue
        step = 1
        while step < count:
            pairs = [(i, i ^ step) for i in range(count)]
            values = values + lax.ppermute(values, axis, pairs)
            step *= 2
    return values


def normalize(values):
    centre_value = jnp.mean(values, axis=-1, keepdims=True)
    centred = values - centre_value
    spread = jnp.mean(centred * centred, axis=-1, keepdims=True)
    inv_dev = lax.rsqrt(spread + 1e-06)
    return (centred * inv_dev, inv_dev)


def depthwise(extended, kernel, reach_cols, **options):
    channels = kernel.shape[-1]
    return lax.conv_general_dilated(
        extended,
        kernel.reshape(kernel.shape[0], kernel.shape[1], 1, channels),
        (1, 1),
        ((0, 0), (reach_cols, reach_cols)),
        dimension_numbers=("NHWC", "HWIO", "NHWC"),
        feature_group_count=channels,
        **options,
    )


def kernel_terms(grad_rows, padded, reach, lanes=128):
    row_count, col_count, channels = grad_rows.shape
    side = 2 * reach + 1
    groups = col_count // 8

    def body(g_ref, x_ref, o_ref):
        for a in range(side):
            for d in range(side):
                acc = jnp.zeros((8, lanes), jnp.float32)
                for h in range(row_count):
                    prod = g_ref[h] * x_ref[h + a, pl.ds(d, col_count), :]
                    acc = acc + prod.reshape(groups, 8, lanes).sum(axis=0)
                o_ref[a, pl.ds(d, 1), :] = acc.sum(axis=0, keepdims=True)

    return pl.pallas_call(
        body,
        grid=(channels // lanes,),
        in_specs=[
            pl.BlockSpec((row_count, col_count, lanes), lambda i: (0, 0, i)),
            pl.BlockSpec(padded.shape[:2] + (lanes,), lambda i: (0, 0, i)),
        ],
        out_specs=pl.BlockSpec((side, side, lanes), lambda i: (0, 0, i)),
        out_shape=jax.ShapeDtypeStruct((side, side, channels), jnp.float32),
    )(grad_rows, padded)

def logsum(scores, axis):
    highest = jnp.max(scores, axis=axis, keepdims=True)
    return jnp.squeeze(highest, axis) + jnp.log(jnp.sum(jnp.exp(scores - highest), axis=axis))


def shards(images, dw_kernel, dw_bias, ln_gain, ln_shift, proj, text, logit_scale):
    batch_dev, row_count, col_count, channels = images.shape
    height = row_count * lax.axis_size("space")
    pixel_count = height * col_count
    batch_count = batch_dev * lax.axis_size("dp")
    reach_rows = dw_kernel.shape[0] // 2
    kernel_float = dw_kernel.astype(jnp.float32)
    extended = with_halo(images, (("space", 1),), reach_rows)
    padded_all = jnp.pad(
        extended.astype(jnp.float32), ((0, 0), (0, 0), (reach_rows, reach_rows), (0, 0))
    )
    conv_out = (
        depthwise(extended, dw_kernel, reach_rows, preferred_element_type=jnp.float32) + dw_bias
    )
    normed, inv_dev = normalize(conv_out)
    pool_part = jnp.sum(normed * ln_gain + ln_shift, axis=(1, 2))
    pool_sum = butterfly_sum(pool_part, ("space",))
    first_row = lax.axis_index("dp") * batch_dev
    packed = jnp.concatenate([pool_sum, text], axis=1)
    table = lax.dynamic_update_slice(
        jnp.zeros((batch_count, packed.shape[1]), jnp.float32), packed, (first_row, 0)
    )
    table = butterfly_sum(table, ("dp",))
    pooled = table[:, :channels] / pixel_count
    all_text = table[:, channels:]
    proj_float = proj.astype(jnp.float32)
    embedded = jnp.dot(pooled, proj_float, precision=lax.Precision.HIGHEST)
    emb_norm = jnp.sqrt(jnp.sum(embedded * embedded, axis=-1, keepdims=True))
    unit_img = embedded / emb_norm
    text_norm = jnp.sqrt(jnp.sum(all_text * all_text, axis=-1, keepdims=True))
    unit_txt = all_text / text_norm
    factor = logit_scale[0]
    scores = factor * jnp.dot(unit_img, unit_txt.T, precision=lax.Precision.HIGHEST)
    row_logsum = logsum(scores, 1)
    col_logsum = logsum(scores, 0)
    identity = jnp.eye(batch_count, dtype=jnp.float32)
    diagonal = jnp.sum(scores * identity, axis=1)
    loss = (jnp.sum(row_logsum - diagonal) + jnp.sum(col_logsum - diagonal)) / (2 * batch_count)
    score_grad = (
        0.5
        * (
            jnp.exp(scores - row_logsum[:, None])
            + jnp.exp(scores - col_logsum[None, :])
        )
        - identity
    )
    unit_img_grad = factor * jnp.dot(score_grad, unit_txt, precision=lax.Precision.HIGHEST)
    unit_txt_grad = factor * jnp.dot(score_grad.T, unit_img, precision=lax.Precision.HIGHEST)
    text_grad_all = (
        unit_txt_grad - unit_txt * jnp.sum(unit_txt * unit_txt_grad, axis=-1, keepdims=True)
    ) / text_norm
    emb_grad_all = (
        unit_img_grad - unit_img * jnp.sum(unit_img * unit_img_grad, axis=-1, keepdims=True)
    ) / emb_norm
    text_grad = lax.dynamic_slice_in_dim(text_grad_all, first_row, batch_dev, axis=0)
    emb_grad = lax.dynamic_slice_in_dim(emb_grad_all, first_row, batch_dev, axis=0)
    weighted = jnp.dot(emb_grad, proj_float.T, precision=lax.Precision.HIGHEST) * ln_gain
    weight_rows = weighted[:, None, None, :]
    weight_mean = jnp.mean(weighted, axis=-1)[:, None, None, None]
    spread_term = jnp.mean(weight_rows * normed, axis=-1, keepdims=True)
    grad_own = inv_dev * (weight_rows - weight_mean - normed * spread_term)
    grad_wide = with_halo(grad_own, (("space", 1),), reach_rows)
    input_grad = depthwise(
        grad_wide, kernel_float[::-1, ::-1], reach_rows, precision=lax.Precision.HIGHEST
    )
    kernel_part = kernel_terms(grad_own[0], padded_all[0], reach_rows)
    for image in range(1, batch_dev):
        kernel_part = kernel_part + kernel_terms(grad_own[image], padded_all[image], reach_rows)
    kernel_grad = butterfly_sum(kernel_part, ("space", "dp")) / pixel_count
    return (loss, input_grad.astype(jnp.bfloat16), kernel_grad, text_grad)


def solution(mesh):
    placed = (P("dp", "space", None, None), P(), P(), P(), P(), P(), P("dp", None), P())
    return jax.shard_map(
        shards,
        mesh=mesh,
        in_specs=placed,
        out_specs=(P(), P("dp", "space", None, None), P(), P("dp", None)),
        check_vma=False,
    )
```

```python
import jax
import jax.numpy as jnp
from jax import lax
from jax.experimental import pallas as pl
from jax.sharding import PartitionSpec as P


def with_halo(block, sides, width):
    for axis, dim in sides:
        count = lax.axis_size(axis)
        forward = [(i, i + 1) for i in range(count - 1)]
        backward = [(target, source) for source, target in forward]
        low = lax.ppermute(
            lax.slice_in_dim(block, block.shape[dim] - width, None, axis=dim), axis, forward
        )
        high = lax.ppermute(lax.slice_in_dim(block, 0, width, axis=dim), axis, backward)
        block = jnp.concatenate([low, block, high], axis=dim)
    return block


def butterfly_sum(values, axes):
    for axis in axes:
        count = lax.axis_size(axis)
        if count & (count - 1):
            values = lax.psum(values, axis)
            continue
        step = 1
        while step < count:
            pairs = [(i, i ^ step) for i in range(count)]
            values = values + lax.ppermute(values, axis, pairs)
            step *= 2
    return values


def halving_sum(values, axes):
    steps = []
    for axis in axes:
        count = lax.axis_size(axis)
        if count & (count - 1):
            return butterfly_sum(values, axes)
        step = 1
        while step < count:
            steps.append((axis, count, step))
            step *= 2
    parts = 1 << len(steps)
    flat = values.reshape(-1)
    size = flat.shape[0]
    padded_size = -(-size // parts) * parts
    chunk = jnp.pad(flat, (0, padded_size - size))
    for axis, count, step in steps:
        pairs = [(i, i ^ step) for i in range(count)]
        upper = (lax.axis_index(axis) // step) % 2 == 1
        half = chunk.shape[0] // 2
        low, high = chunk[:half], chunk[half:]
        keep = jnp.where(upper, high, low)
        give = jnp.where(upper, low, high)
        chunk = keep + lax.ppermute(give, axis, pairs)
    for axis, count, step in reversed(steps):
        pairs = [(i, i ^ step) for i in range(count)]
        upper = (lax.axis_index(axis) // step) % 2 == 1
        other = lax.ppermute(chunk, axis, pairs)
        chunk = jnp.where(
            upper, jnp.concatenate([other, chunk]), jnp.concatenate([chunk, other])
        )
    return chunk[:size].reshape(values.shape)


def normalize(values):
    centre_value = jnp.mean(values, axis=-1, keepdims=True)
    centred = values - centre_value
    spread = jnp.mean(centred * centred, axis=-1, keepdims=True)
    inv_dev = lax.rsqrt(spread + 1e-06)
    return (centred * inv_dev, inv_dev)


def depthwise(extended, kernel, reach_cols, **options):
    channels = kernel.shape[-1]
    return lax.conv_general_dilated(
        extended,
        kernel.reshape(kernel.shape[0], kernel.shape[1], 1, channels),
        (1, 1),
        ((0, 0), (reach_cols, reach_cols)),
        dimension_numbers=("NHWC", "HWIO", "NHWC"),
        feature_group_count=channels,
        **options,
    )


def kernel_terms(grad_rows, padded, reach, lanes=128):
    row_count, col_count, channels = grad_rows.shape
    side = 2 * reach + 1
    groups = col_count // 8

    def body(g_ref, x_ref, o_ref):
        for a in range(side):
            for d in range(side):
                acc = jnp.zeros((8, lanes), jnp.float32)
                for h in range(row_count):
                    prod = g_ref[h] * x_ref[h + a, pl.ds(d, col_count), :]
                    acc = acc + prod.reshape(groups, 8, lanes).sum(axis=0)
                o_ref[a, pl.ds(d, 1), :] = acc.sum(axis=0, keepdims=True)

    return pl.pallas_call(
        body,
        grid=(channels // lanes,),
        in_specs=[
            pl.BlockSpec((row_count, col_count, lanes), lambda i: (0, 0, i)),
            pl.BlockSpec(padded.shape[:2] + (lanes,), lambda i: (0, 0, i)),
        ],
        out_specs=pl.BlockSpec((side, side, lanes), lambda i: (0, 0, i)),
        out_shape=jax.ShapeDtypeStruct((side, side, channels), jnp.float32),
    )(grad_rows, padded)

def logsum(scores, axis):
    highest = jnp.max(scores, axis=axis, keepdims=True)
    return jnp.squeeze(highest, axis) + jnp.log(jnp.sum(jnp.exp(scores - highest), axis=axis))


def shards(images, dw_kernel, dw_bias, ln_gain, ln_shift, proj, text, logit_scale):
    batch_dev, row_count, col_count, channels = images.shape
    height = row_count * lax.axis_size("space")
    pixel_count = height * col_count
    batch_count = batch_dev * lax.axis_size("dp")
    reach_rows = dw_kernel.shape[0] // 2
    kernel_float = dw_kernel.astype(jnp.float32)
    extended = with_halo(images, (("space", 1),), reach_rows)
    padded_all = jnp.pad(
        extended.astype(jnp.float32), ((0, 0), (0, 0), (reach_rows, reach_rows), (0, 0))
    )
    conv_out = (
        depthwise(extended, dw_kernel, reach_rows, preferred_element_type=jnp.float32) + dw_bias
    )
    normed, inv_dev = normalize(conv_out)
    pool_part = jnp.sum(normed * ln_gain + ln_shift, axis=(1, 2))
    pool_sum = butterfly_sum(pool_part, ("space",))
    first_row = lax.axis_index("dp") * batch_dev
    packed = jnp.concatenate([pool_sum, text], axis=1)
    table = lax.dynamic_update_slice(
        jnp.zeros((batch_count, packed.shape[1]), jnp.float32), packed, (first_row, 0)
    )
    table = butterfly_sum(table, ("dp",))
    pooled = table[:, :channels] / pixel_count
    all_text = table[:, channels:]
    proj_float = proj.astype(jnp.float32)
    embedded = jnp.dot(pooled, proj_float, precision=lax.Precision.HIGHEST)
    emb_norm = jnp.sqrt(jnp.sum(embedded * embedded, axis=-1, keepdims=True))
    unit_img = embedded / emb_norm
    text_norm = jnp.sqrt(jnp.sum(all_text * all_text, axis=-1, keepdims=True))
    unit_txt = all_text / text_norm
    factor = logit_scale[0]
    scores = factor * jnp.dot(unit_img, unit_txt.T, precision=lax.Precision.HIGHEST)
    row_logsum = logsum(scores, 1)
    col_logsum = logsum(scores, 0)
    identity = jnp.eye(batch_count, dtype=jnp.float32)
    diagonal = jnp.sum(scores * identity, axis=1)
    loss = (jnp.sum(row_logsum - diagonal) + jnp.sum(col_logsum - diagonal)) / (2 * batch_count)
    score_grad = (
        0.5
        * (
            jnp.exp(scores - row_logsum[:, None])
            + jnp.exp(scores - col_logsum[None, :])
        )
        - identity
    )
    unit_img_grad = factor * jnp.dot(score_grad, unit_txt, precision=lax.Precision.HIGHEST)
    unit_txt_grad = factor * jnp.dot(score_grad.T, unit_img, precision=lax.Precision.HIGHEST)
    text_grad_all = (
        unit_txt_grad - unit_txt * jnp.sum(unit_txt * unit_txt_grad, axis=-1, keepdims=True)
    ) / text_norm
    emb_grad_all = (
        unit_img_grad - unit_img * jnp.sum(unit_img * unit_img_grad, axis=-1, keepdims=True)
    ) / emb_norm
    text_grad = lax.dynamic_slice_in_dim(text_grad_all, first_row, batch_dev, axis=0)
    emb_grad = lax.dynamic_slice_in_dim(emb_grad_all, first_row, batch_dev, axis=0)
    weighted = jnp.dot(emb_grad, proj_float.T, precision=lax.Precision.HIGHEST) * ln_gain
    weight_rows = weighted[:, None, None, :]
    weight_mean = jnp.mean(weighted, axis=-1)[:, None, None, None]
    spread_term = jnp.mean(weight_rows * normed, axis=-1, keepdims=True)
    grad_own = inv_dev * (weight_rows - weight_mean - normed * spread_term)
    grad_wide = with_halo(grad_own, (("space", 1),), reach_rows)
    input_grad = depthwise(
        grad_wide, kernel_float[::-1, ::-1], reach_rows, precision=lax.Precision.HIGHEST
    )
    kernel_part = kernel_terms(grad_own[0], padded_all[0], reach_rows)
    for image in range(1, batch_dev):
        kernel_part = kernel_part + kernel_terms(grad_own[image], padded_all[image], reach_rows)
    kernel_grad = halving_sum(kernel_part, ("space", "dp")) / pixel_count
    return (loss, input_grad.astype(jnp.bfloat16), kernel_grad, text_grad)


def solution(mesh):
    placed = (P("dp", "space", None, None), P(), P(), P(), P(), P(), P("dp", None), P())
    return jax.shard_map(
        shards,
        mesh=mesh,
        in_specs=placed,
        out_specs=(P(), P("dp", "space", None, None), P(), P("dp", None)),
        check_vma=False,
    )
```

```python
import jax
import jax.numpy as jnp
from jax import lax
from jax.experimental import pallas as pl
from jax.sharding import PartitionSpec as P


def with_halo(block, sides, width):
    for axis, dim in sides:
        count = lax.axis_size(axis)
        forward = [(i, i + 1) for i in range(count - 1)]
        backward = [(target, source) for source, target in forward]
        low = lax.ppermute(
            lax.slice_in_dim(block, block.shape[dim] - width, None, axis=dim), axis, forward
        )
        high = lax.ppermute(lax.slice_in_dim(block, 0, width, axis=dim), axis, backward)
        block = jnp.concatenate([low, block, high], axis=dim)
    return block


def butterfly_sum(values, axes):
    for axis in axes:
        count = lax.axis_size(axis)
        if count & (count - 1):
            values = lax.psum(values, axis)
            continue
        step = 1
        while step < count:
            pairs = [(i, i ^ step) for i in range(count)]
            values = values + lax.ppermute(values, axis, pairs)
            step *= 2
    return values


def halving_sum(values, axes):
    steps = []
    for axis in axes:
        count = lax.axis_size(axis)
        if count & (count - 1):
            return butterfly_sum(values, axes)
        step = 1
        while step < count:
            steps.append((axis, count, step))
            step *= 2
    parts = 1 << len(steps)
    flat = values.reshape(-1)
    size = flat.shape[0]
    padded_size = -(-size // parts) * parts
    chunk = jnp.pad(flat, (0, padded_size - size))
    for axis, count, step in steps:
        pairs = [(i, i ^ step) for i in range(count)]
        upper = (lax.axis_index(axis) // step) % 2 == 1
        half = chunk.shape[0] // 2
        low, high = chunk[:half], chunk[half:]
        keep = jnp.where(upper, high, low)
        give = jnp.where(upper, low, high)
        chunk = keep + lax.ppermute(give, axis, pairs)
    for axis, count, step in reversed(steps):
        pairs = [(i, i ^ step) for i in range(count)]
        upper = (lax.axis_index(axis) // step) % 2 == 1
        other = lax.ppermute(chunk, axis, pairs)
        chunk = jnp.where(
            upper, jnp.concatenate([other, chunk]), jnp.concatenate([chunk, other])
        )
    return chunk[:size].reshape(values.shape)


def normalize(values):
    centre_value = jnp.mean(values, axis=-1, keepdims=True)
    centred = values - centre_value
    spread = jnp.mean(centred * centred, axis=-1, keepdims=True)
    inv_dev = lax.rsqrt(spread + 1e-06)
    return (centred * inv_dev, inv_dev)


def depthwise(extended, kernel, reach_cols, **options):
    channels = kernel.shape[-1]
    return lax.conv_general_dilated(
        extended,
        kernel.reshape(kernel.shape[0], kernel.shape[1], 1, channels),
        (1, 1),
        ((0, 0), (reach_cols, reach_cols)),
        dimension_numbers=("NHWC", "HWIO", "NHWC"),
        feature_group_count=channels,
        **options,
    )


def kernel_terms(grad_rows, padded, reach, lanes=128):
    row_count, col_count, channels = grad_rows.shape
    side = 2 * reach + 1
    groups = col_count // 8

    def body(g_ref, x_ref, o_ref):
        for a in range(side):
            for d in range(side):
                acc = jnp.zeros((8, lanes), jnp.float32)
                for h in range(row_count):
                    prod = g_ref[h] * x_ref[h + a, pl.ds(d, col_count), :]
                    acc = acc + prod.reshape(groups, 8, lanes).sum(axis=0)
                o_ref[a, pl.ds(d, 1), :] = acc.sum(axis=0, keepdims=True)

    return pl.pallas_call(
        body,
        grid=(channels // lanes,),
        in_specs=[
            pl.BlockSpec((row_count, col_count, lanes), lambda i: (0, 0, i)),
            pl.BlockSpec(padded.shape[:2] + (lanes,), lambda i: (0, 0, i)),
        ],
        out_specs=pl.BlockSpec((side, side, lanes), lambda i: (0, 0, i)),
        out_shape=jax.ShapeDtypeStruct((side, side, channels), jnp.float32),
    )(grad_rows, padded)

def input_terms(padded, kernel, row_count, lanes=128):
    side = kernel.shape[0]
    col_count = padded.shape[1] - side + 1
    channels = padded.shape[2]

    def body(x_ref, k_ref, o_ref):
        for h in range(row_count):
            acc = jnp.zeros((col_count, lanes), jnp.float32)
            for a in range(side):
                for d in range(side):
                    acc = acc + k_ref[a, pl.ds(d, 1), :] * x_ref[h + a, pl.ds(d, col_count), :]
            o_ref[h] = acc.astype(o_ref.dtype)

    return pl.pallas_call(
        body,
        grid=(channels // lanes,),
        in_specs=[
            pl.BlockSpec(padded.shape[:2] + (lanes,), lambda i: (0, 0, i)),
            pl.BlockSpec((side, side, lanes), lambda i: (0, 0, i)),
        ],
        out_specs=pl.BlockSpec((row_count, col_count, lanes), lambda i: (0, 0, i)),
        out_shape=jax.ShapeDtypeStruct((row_count, col_count, channels), jnp.bfloat16),
    )(padded, kernel)

def logsum(scores, axis):
    highest = jnp.max(scores, axis=axis, keepdims=True)
    return jnp.squeeze(highest, axis) + jnp.log(jnp.sum(jnp.exp(scores - highest), axis=axis))


def shards(images, dw_kernel, dw_bias, ln_gain, ln_shift, proj, text, logit_scale):
    batch_dev, row_count, col_count, channels = images.shape
    height = row_count * lax.axis_size("space")
    pixel_count = height * col_count
    batch_count = batch_dev * lax.axis_size("dp")
    reach_rows = dw_kernel.shape[0] // 2
    kernel_float = dw_kernel.astype(jnp.float32)
    extended = with_halo(images, (("space", 1),), reach_rows)
    padded_all = jnp.pad(
        extended.astype(jnp.float32), ((0, 0), (0, 0), (reach_rows, reach_rows), (0, 0))
    )
    conv_out = (
        depthwise(extended, dw_kernel, reach_rows, preferred_element_type=jnp.float32) + dw_bias
    )
    normed, inv_dev = normalize(conv_out)
    pool_part = jnp.sum(normed * ln_gain + ln_shift, axis=(1, 2))
    pool_sum = butterfly_sum(pool_part, ("space",))
    first_row = lax.axis_index("dp") * batch_dev
    packed = jnp.concatenate([pool_sum, text], axis=1)
    table = lax.dynamic_update_slice(
        jnp.zeros((batch_count, packed.shape[1]), jnp.float32), packed, (first_row, 0)
    )
    table = butterfly_sum(table, ("dp",))
    pooled = table[:, :channels] / pixel_count
    all_text = table[:, channels:]
    proj_float = proj.astype(jnp.float32)
    embedded = jnp.dot(pooled, proj_float, precision=lax.Precision.HIGHEST)
    emb_norm = jnp.sqrt(jnp.sum(embedded * embedded, axis=-1, keepdims=True))
    unit_img = embedded / emb_norm
    text_norm = jnp.sqrt(jnp.sum(all_text * all_text, axis=-1, keepdims=True))
    unit_txt = all_text / text_norm
    factor = logit_scale[0]
    scores = factor * jnp.dot(unit_img, unit_txt.T, precision=lax.Precision.HIGHEST)
    row_logsum = logsum(scores, 1)
    col_logsum = logsum(scores, 0)
    identity = jnp.eye(batch_count, dtype=jnp.float32)
    diagonal = jnp.sum(scores * identity, axis=1)
    loss = (jnp.sum(row_logsum - diagonal) + jnp.sum(col_logsum - diagonal)) / (2 * batch_count)
    score_grad = (
        0.5
        * (
            jnp.exp(scores - row_logsum[:, None])
            + jnp.exp(scores - col_logsum[None, :])
        )
        - identity
    )
    unit_img_grad = factor * jnp.dot(score_grad, unit_txt, precision=lax.Precision.HIGHEST)
    unit_txt_grad = factor * jnp.dot(score_grad.T, unit_img, precision=lax.Precision.HIGHEST)
    text_grad_all = (
        unit_txt_grad - unit_txt * jnp.sum(unit_txt * unit_txt_grad, axis=-1, keepdims=True)
    ) / text_norm
    emb_grad_all = (
        unit_img_grad - unit_img * jnp.sum(unit_img * unit_img_grad, axis=-1, keepdims=True)
    ) / emb_norm
    text_grad = lax.dynamic_slice_in_dim(text_grad_all, first_row, batch_dev, axis=0)
    emb_grad = lax.dynamic_slice_in_dim(emb_grad_all, first_row, batch_dev, axis=0)
    weighted = jnp.dot(emb_grad, proj_float.T, precision=lax.Precision.HIGHEST) * ln_gain
    weight_rows = weighted[:, None, None, :]
    weight_mean = jnp.mean(weighted, axis=-1)[:, None, None, None]
    spread_term = jnp.mean(weight_rows * normed, axis=-1, keepdims=True)
    grad_own = inv_dev * (weight_rows - weight_mean - normed * spread_term)
    grad_wide = with_halo(grad_own, (("space", 1),), reach_rows)
    grad_pad = jnp.pad(grad_wide, ((0, 0), (0, 0), (reach_rows, reach_rows), (0, 0)))
    flipped = kernel_float[::-1, ::-1]
    input_grad = jnp.stack(
        [input_terms(grad_pad[image], flipped, row_count) for image in range(batch_dev)]
    )
    kernel_part = kernel_terms(grad_own[0], padded_all[0], reach_rows)
    for image in range(1, batch_dev):
        kernel_part = kernel_part + kernel_terms(grad_own[image], padded_all[image], reach_rows)
    kernel_grad = halving_sum(kernel_part, ("space", "dp")) / pixel_count
    return (loss, input_grad.astype(jnp.bfloat16), kernel_grad, text_grad)


def solution(mesh):
    placed = (P("dp", "space", None, None), P(), P(), P(), P(), P(), P("dp", None), P())
    return jax.shard_map(
        shards,
        mesh=mesh,
        in_specs=placed,
        out_specs=(P(), P("dp", "space", None, None), P(), P("dp", None)),
        check_vma=False,
    )
```

```python
import jax
import jax.numpy as jnp
from jax import lax
from jax.experimental import pallas as pl
from jax.sharding import PartitionSpec as P


def with_halo(block, sides, width):
    for axis, dim in sides:
        count = lax.axis_size(axis)
        forward = [(i, i + 1) for i in range(count - 1)]
        backward = [(target, source) for source, target in forward]
        low = lax.ppermute(
            lax.slice_in_dim(block, block.shape[dim] - width, None, axis=dim), axis, forward
        )
        high = lax.ppermute(lax.slice_in_dim(block, 0, width, axis=dim), axis, backward)
        block = jnp.concatenate([low, block, high], axis=dim)
    return block


def butterfly_sum(values, axes):
    for axis in axes:
        count = lax.axis_size(axis)
        if count & (count - 1):
            values = lax.psum(values, axis)
            continue
        step = 1
        while step < count:
            pairs = [(i, i ^ step) for i in range(count)]
            values = values + lax.ppermute(values, axis, pairs)
            step *= 2
    return values


def halving_sum(values, axes, split_steps):
    steps = []
    for axis in axes:
        count = lax.axis_size(axis)
        if count & (count - 1):
            return butterfly_sum(values, axes)
        step = 1
        while step < count:
            steps.append((axis, count, step))
            step *= 2
    split_steps = min(split_steps, len(steps))
    parts = 1 << split_steps
    flat = values.reshape(-1)
    size = flat.shape[0]
    padded_size = -(-size // parts) * parts
    chunk = jnp.pad(flat, (0, padded_size - size))
    for axis, count, step in steps[:split_steps]:
        pairs = [(i, i ^ step) for i in range(count)]
        upper = (lax.axis_index(axis) // step) % 2 == 1
        half = chunk.shape[0] // 2
        low, high = chunk[:half], chunk[half:]
        keep = jnp.where(upper, high, low)
        give = jnp.where(upper, low, high)
        chunk = keep + lax.ppermute(give, axis, pairs)
    for axis, count, step in steps[split_steps:]:
        pairs = [(i, i ^ step) for i in range(count)]
        chunk = chunk + lax.ppermute(chunk, axis, pairs)
    for axis, count, step in reversed(steps[:split_steps]):
        pairs = [(i, i ^ step) for i in range(count)]
        upper = (lax.axis_index(axis) // step) % 2 == 1
        other = lax.ppermute(chunk, axis, pairs)
        chunk = jnp.where(
            upper, jnp.concatenate([other, chunk]), jnp.concatenate([chunk, other])
        )
    return chunk[:size].reshape(values.shape)


def normalize(values):
    centre_value = jnp.mean(values, axis=-1, keepdims=True)
    centred = values - centre_value
    spread = jnp.mean(centred * centred, axis=-1, keepdims=True)
    inv_dev = lax.rsqrt(spread + 1e-06)
    return (centred * inv_dev, inv_dev)


def depthwise(extended, kernel, reach_cols, **options):
    channels = kernel.shape[-1]
    return lax.conv_general_dilated(
        extended,
        kernel.reshape(kernel.shape[0], kernel.shape[1], 1, channels),
        (1, 1),
        ((0, 0), (reach_cols, reach_cols)),
        dimension_numbers=("NHWC", "HWIO", "NHWC"),
        feature_group_count=channels,
        **options,
    )


def kernel_terms(grad_rows, padded, reach, lanes=128):
    row_count, col_count, channels = grad_rows.shape
    side = 2 * reach + 1
    groups = col_count // 8

    def body(g_ref, x_ref, o_ref):
        for a in range(side):
            for d in range(side):
                acc = jnp.zeros((8, lanes), jnp.float32)
                for h in range(row_count):
                    prod = g_ref[h] * x_ref[h + a, pl.ds(d, col_count), :]
                    acc = acc + prod.reshape(groups, 8, lanes).sum(axis=0)
                o_ref[a, pl.ds(d, 1), :] = acc.sum(axis=0, keepdims=True)

    return pl.pallas_call(
        body,
        grid=(channels // lanes,),
        in_specs=[
            pl.BlockSpec((row_count, col_count, lanes), lambda i: (0, 0, i)),
            pl.BlockSpec(padded.shape[:2] + (lanes,), lambda i: (0, 0, i)),
        ],
        out_specs=pl.BlockSpec((side, side, lanes), lambda i: (0, 0, i)),
        out_shape=jax.ShapeDtypeStruct((side, side, channels), jnp.float32),
    )(grad_rows, padded)

def input_terms(padded, kernel, row_count, lanes=128):
    side = kernel.shape[0]
    col_count = padded.shape[1] - side + 1
    channels = padded.shape[2]

    def body(x_ref, k_ref, o_ref):
        for h in range(row_count):
            acc = jnp.zeros((col_count, lanes), jnp.float32)
            for a in range(side):
                for d in range(side):
                    acc = acc + k_ref[a, pl.ds(d, 1), :] * x_ref[h + a, pl.ds(d, col_count), :]
            o_ref[h] = acc.astype(o_ref.dtype)

    return pl.pallas_call(
        body,
        grid=(channels // lanes,),
        in_specs=[
            pl.BlockSpec(padded.shape[:2] + (lanes,), lambda i: (0, 0, i)),
            pl.BlockSpec((side, side, lanes), lambda i: (0, 0, i)),
        ],
        out_specs=pl.BlockSpec((row_count, col_count, lanes), lambda i: (0, 0, i)),
        out_shape=jax.ShapeDtypeStruct((row_count, col_count, channels), jnp.bfloat16),
    )(padded, kernel)

def logsum(scores, axis):
    highest = jnp.max(scores, axis=axis, keepdims=True)
    return jnp.squeeze(highest, axis) + jnp.log(jnp.sum(jnp.exp(scores - highest), axis=axis))


def shards(images, dw_kernel, dw_bias, ln_gain, ln_shift, proj, text, logit_scale):
    batch_dev, row_count, col_count, channels = images.shape
    height = row_count * lax.axis_size("space")
    pixel_count = height * col_count
    batch_count = batch_dev * lax.axis_size("dp")
    reach_rows = dw_kernel.shape[0] // 2
    kernel_float = dw_kernel.astype(jnp.float32)
    extended = with_halo(images, (("space", 1),), reach_rows)
    padded_all = jnp.pad(
        extended.astype(jnp.float32), ((0, 0), (0, 0), (reach_rows, reach_rows), (0, 0))
    )
    conv_out = (
        depthwise(extended, dw_kernel, reach_rows, preferred_element_type=jnp.float32) + dw_bias
    )
    normed, inv_dev = normalize(conv_out)
    pool_part = jnp.sum(normed * ln_gain + ln_shift, axis=(1, 2))
    pool_sum = butterfly_sum(pool_part, ("space",))
    first_row = lax.axis_index("dp") * batch_dev
    packed = jnp.concatenate([pool_sum, text], axis=1)
    table = lax.dynamic_update_slice(
        jnp.zeros((batch_count, packed.shape[1]), jnp.float32), packed, (first_row, 0)
    )
    table = butterfly_sum(table, ("dp",))
    pooled = table[:, :channels] / pixel_count
    all_text = table[:, channels:]
    proj_float = proj.astype(jnp.float32)
    embedded = jnp.dot(pooled, proj_float, precision=lax.Precision.HIGHEST)
    emb_norm = jnp.sqrt(jnp.sum(embedded * embedded, axis=-1, keepdims=True))
    unit_img = embedded / emb_norm
    text_norm = jnp.sqrt(jnp.sum(all_text * all_text, axis=-1, keepdims=True))
    unit_txt = all_text / text_norm
    factor = logit_scale[0]
    scores = factor * jnp.dot(unit_img, unit_txt.T, precision=lax.Precision.HIGHEST)
    row_logsum = logsum(scores, 1)
    col_logsum = logsum(scores, 0)
    identity = jnp.eye(batch_count, dtype=jnp.float32)
    diagonal = jnp.sum(scores * identity, axis=1)
    loss = (jnp.sum(row_logsum - diagonal) + jnp.sum(col_logsum - diagonal)) / (2 * batch_count)
    score_grad = (
        0.5
        * (
            jnp.exp(scores - row_logsum[:, None])
            + jnp.exp(scores - col_logsum[None, :])
        )
        - identity
    )
    unit_img_grad = factor * jnp.dot(score_grad, unit_txt, precision=lax.Precision.HIGHEST)
    unit_txt_grad = factor * jnp.dot(score_grad.T, unit_img, precision=lax.Precision.HIGHEST)
    text_grad_all = (
        unit_txt_grad - unit_txt * jnp.sum(unit_txt * unit_txt_grad, axis=-1, keepdims=True)
    ) / text_norm
    emb_grad_all = (
        unit_img_grad - unit_img * jnp.sum(unit_img * unit_img_grad, axis=-1, keepdims=True)
    ) / emb_norm
    text_grad = lax.dynamic_slice_in_dim(text_grad_all, first_row, batch_dev, axis=0)
    emb_grad = lax.dynamic_slice_in_dim(emb_grad_all, first_row, batch_dev, axis=0)
    weighted = jnp.dot(emb_grad, proj_float.T, precision=lax.Precision.HIGHEST) * ln_gain
    weight_rows = weighted[:, None, None, :]
    weight_mean = jnp.mean(weighted, axis=-1)[:, None, None, None]
    spread_term = jnp.mean(weight_rows * normed, axis=-1, keepdims=True)
    grad_own = inv_dev * (weight_rows - weight_mean - normed * spread_term)
    grad_wide = with_halo(grad_own, (("space", 1),), reach_rows)
    grad_pad = jnp.pad(grad_wide, ((0, 0), (0, 0), (reach_rows, reach_rows), (0, 0)))
    flipped = kernel_float[::-1, ::-1]
    input_grad = jnp.stack(
        [input_terms(grad_pad[image], flipped, row_count) for image in range(batch_dev)]
    )
    kernel_part = kernel_terms(grad_own[0], padded_all[0], reach_rows)
    for image in range(1, batch_dev):
        kernel_part = kernel_part + kernel_terms(grad_own[image], padded_all[image], reach_rows)
    kernel_part, input_grad = lax.optimization_barrier((kernel_part, input_grad))
    kernel_grad = halving_sum(kernel_part, ("space", "dp"), 3) / pixel_count
    return (loss, input_grad.astype(jnp.bfloat16), kernel_grad, text_grad)


def solution(mesh):
    placed = (P("dp", "space", None, None), P(), P(), P(), P(), P(), P("dp", None), P())
    return jax.shard_map(
        shards,
        mesh=mesh,
        in_specs=placed,
        out_specs=(P(), P("dp", "space", None, None), P(), P("dp", None)),
        check_vma=False,
    )
```

```python
import jax
import jax.numpy as jnp
from jax import lax
from jax.experimental import pallas as pl
from jax.sharding import PartitionSpec as P


def with_halo(block, sides, width):
    for axis, dim in sides:
        count = lax.axis_size(axis)
        forward = [(i, i + 1) for i in range(count - 1)]
        backward = [(target, source) for source, target in forward]
        low = lax.ppermute(
            lax.slice_in_dim(block, block.shape[dim] - width, None, axis=dim), axis, forward
        )
        high = lax.ppermute(lax.slice_in_dim(block, 0, width, axis=dim), axis, backward)
        block = jnp.concatenate([low, block, high], axis=dim)
    return block


def butterfly_sum(values, axes, riders=None):
    riders_done = None
    for axis in axes:
        count = lax.axis_size(axis)
        if count & (count - 1):
            values = lax.psum(values, axis)
            continue
        step = 1
        while step < count:
            pairs = [(i, i ^ step) for i in range(count)]
            received = lax.ppermute(values, axis, pairs)
            if riders is not None:
                received, riders = lax.optimization_barrier((received, riders))
                riders_done = riders
                riders = None
            values = values + received
            step *= 2
    return values if riders_done is None else (values, riders_done)


def halving_sum(values, axes, split_steps, riders):
    steps = []
    for axis in axes:
        count = lax.axis_size(axis)
        if count & (count - 1):
            return butterfly_sum(values, axes)
        step = 1
        while step < count:
            steps.append((axis, count, step))
            step *= 2
    split_steps = min(split_steps, len(steps))
    riders_done = None
    parts = 1 << split_steps
    flat = values.reshape(-1)
    size = flat.shape[0]
    padded_size = -(-size // parts) * parts
    chunk = jnp.pad(flat, (0, padded_size - size))
    for axis, count, step in steps[:split_steps]:
        pairs = [(i, i ^ step) for i in range(count)]
        upper = (lax.axis_index(axis) // step) % 2 == 1
        half = chunk.shape[0] // 2
        low, high = chunk[:half], chunk[half:]
        keep = jnp.where(upper, high, low)
        give = jnp.where(upper, low, high)
        received = lax.ppermute(give, axis, pairs)
        if riders is not None:
            received, riders_done = lax.optimization_barrier((received, riders))
            riders = None
        chunk = keep + received
    for axis, count, step in steps[split_steps:]:
        pairs = [(i, i ^ step) for i in range(count)]
        chunk = chunk + lax.ppermute(chunk, axis, pairs)
    for axis, count, step in reversed(steps[:split_steps]):
        pairs = [(i, i ^ step) for i in range(count)]
        upper = (lax.axis_index(axis) // step) % 2 == 1
        other = lax.ppermute(chunk, axis, pairs)
        chunk = jnp.where(
            upper, jnp.concatenate([other, chunk]), jnp.concatenate([chunk, other])
        )
    return chunk[:size].reshape(values.shape), riders_done


def normalize(values):
    centre_value = jnp.mean(values, axis=-1, keepdims=True)
    centred = values - centre_value
    spread = jnp.mean(centred * centred, axis=-1, keepdims=True)
    inv_dev = lax.rsqrt(spread + 1e-06)
    return (centred * inv_dev, inv_dev)


def depthwise(extended, kernel, reach_cols, **options):
    channels = kernel.shape[-1]
    return lax.conv_general_dilated(
        extended,
        kernel.reshape(kernel.shape[0], kernel.shape[1], 1, channels),
        (1, 1),
        ((0, 0), (reach_cols, reach_cols)),
        dimension_numbers=("NHWC", "HWIO", "NHWC"),
        feature_group_count=channels,
        **options,
    )


def kernel_terms(grad_rows, padded, reach, lanes=128):
    row_count, col_count, channels = grad_rows.shape
    side = 2 * reach + 1
    groups = col_count // 8

    def body(g_ref, x_ref, o_ref):
        for a in range(side):
            for d in range(side):
                acc = jnp.zeros((8, lanes), jnp.float32)
                for h in range(row_count):
                    prod = g_ref[h] * x_ref[h + a, pl.ds(d, col_count), :]
                    acc = acc + prod.reshape(groups, 8, lanes).sum(axis=0)
                o_ref[a, pl.ds(d, 1), :] = acc.sum(axis=0, keepdims=True)

    return pl.pallas_call(
        body,
        grid=(channels // lanes,),
        in_specs=[
            pl.BlockSpec((row_count, col_count, lanes), lambda i: (0, 0, i)),
            pl.BlockSpec(padded.shape[:2] + (lanes,), lambda i: (0, 0, i)),
        ],
        out_specs=pl.BlockSpec((side, side, lanes), lambda i: (0, 0, i)),
        out_shape=jax.ShapeDtypeStruct((side, side, channels), jnp.float32),
    )(grad_rows, padded)

def input_terms(padded, kernel, row_count, lanes=128):
    side = kernel.shape[0]
    col_count = padded.shape[1] - side + 1
    channels = padded.shape[2]

    def body(x_ref, k_ref, o_ref):
        for h in range(row_count):
            acc = jnp.zeros((col_count, lanes), jnp.float32)
            for a in range(side):
                for d in range(side):
                    weight = k_ref[side - 1 - a, pl.ds(side - 1 - d, 1), :]
                    acc = acc + weight * x_ref[h + a, pl.ds(d, col_count), :]
            o_ref[h] = acc.astype(o_ref.dtype)

    return pl.pallas_call(
        body,
        grid=(channels // lanes,),
        in_specs=[
            pl.BlockSpec(padded.shape[:2] + (lanes,), lambda i: (0, 0, i)),
            pl.BlockSpec((side, side, lanes), lambda i: (0, 0, i)),
        ],
        out_specs=pl.BlockSpec((row_count, col_count, lanes), lambda i: (0, 0, i)),
        out_shape=jax.ShapeDtypeStruct((row_count, col_count, channels), jnp.bfloat16),
    )(padded, kernel)

def logsum(scores, axis):
    highest = jnp.max(scores, axis=axis, keepdims=True)
    return jnp.squeeze(highest, axis) + jnp.log(jnp.sum(jnp.exp(scores - highest), axis=axis))


def shards(images, dw_kernel, dw_bias, ln_gain, ln_shift, proj, text, logit_scale):
    batch_dev, row_count, col_count, channels = images.shape
    height = row_count * lax.axis_size("space")
    pixel_count = height * col_count
    batch_count = batch_dev * lax.axis_size("dp")
    reach_rows = dw_kernel.shape[0] // 2
    kernel_float = dw_kernel.astype(jnp.float32)
    extended = with_halo(images, (("space", 1),), reach_rows)
    padded_all = jnp.pad(
        extended.astype(jnp.float32), ((0, 0), (0, 0), (reach_rows, reach_rows), (0, 0))
    )
    conv_out = (
        depthwise(extended, dw_kernel, reach_rows, preferred_element_type=jnp.float32) + dw_bias
    )
    normed, inv_dev = normalize(conv_out)
    pool_part = jnp.sum(normed * ln_gain + ln_shift, axis=(1, 2))
    pool_sum, padded_all = butterfly_sum(pool_part, ("space",), riders=padded_all)
    first_row = lax.axis_index("dp") * batch_dev
    packed = jnp.concatenate([pool_sum, text], axis=1)
    table = lax.dynamic_update_slice(
        jnp.zeros((batch_count, packed.shape[1]), jnp.float32), packed, (first_row, 0)
    )
    table = butterfly_sum(table, ("dp",))
    pooled = table[:, :channels] / pixel_count
    all_text = table[:, channels:]
    proj_float = proj.astype(jnp.float32)
    embedded = jnp.dot(pooled, proj_float, precision=lax.Precision.HIGHEST)
    emb_norm = jnp.sqrt(jnp.sum(embedded * embedded, axis=-1, keepdims=True))
    unit_img = embedded / emb_norm
    text_norm = jnp.sqrt(jnp.sum(all_text * all_text, axis=-1, keepdims=True))
    unit_txt = all_text / text_norm
    factor = logit_scale[0]
    scores = factor * jnp.dot(unit_img, unit_txt.T, precision=lax.Precision.HIGHEST)
    row_logsum = logsum(scores, 1)
    col_logsum = logsum(scores, 0)
    identity = jnp.eye(batch_count, dtype=jnp.float32)
    diagonal = jnp.sum(scores * identity, axis=1)
    loss = (jnp.sum(row_logsum - diagonal) + jnp.sum(col_logsum - diagonal)) / (2 * batch_count)
    score_grad = (
        0.5
        * (
            jnp.exp(scores - row_logsum[:, None])
            + jnp.exp(scores - col_logsum[None, :])
        )
        - identity
    )
    unit_img_grad = factor * jnp.dot(score_grad, unit_txt, precision=lax.Precision.HIGHEST)
    unit_txt_grad = factor * jnp.dot(score_grad.T, unit_img, precision=lax.Precision.HIGHEST)
    text_grad_all = (
        unit_txt_grad - unit_txt * jnp.sum(unit_txt * unit_txt_grad, axis=-1, keepdims=True)
    ) / text_norm
    emb_grad_all = (
        unit_img_grad - unit_img * jnp.sum(unit_img * unit_img_grad, axis=-1, keepdims=True)
    ) / emb_norm
    text_grad = lax.dynamic_slice_in_dim(text_grad_all, first_row, batch_dev, axis=0)
    emb_grad = lax.dynamic_slice_in_dim(emb_grad_all, first_row, batch_dev, axis=0)
    weighted = jnp.dot(emb_grad, proj_float.T, precision=lax.Precision.HIGHEST) * ln_gain
    weight_rows = weighted[:, None, None, :]
    weight_mean = jnp.mean(weighted, axis=-1)[:, None, None, None]
    spread_term = jnp.mean(weight_rows * normed, axis=-1, keepdims=True)
    grad_own = inv_dev * (weight_rows - weight_mean - normed * spread_term)
    grad_wide = with_halo(grad_own, (("space", 1),), reach_rows)
    grad_pad = jnp.pad(grad_wide, ((0, 0), (0, 0), (reach_rows, reach_rows), (0, 0)))
    input_grad = jnp.stack(
        [input_terms(grad_pad[image], kernel_float, row_count) for image in range(batch_dev)]
    )
    kernel_part = kernel_terms(grad_own[0], padded_all[0], reach_rows)
    for image in range(1, batch_dev):
        kernel_part = kernel_part + kernel_terms(grad_own[image], padded_all[image], reach_rows)
    kernel_sum, input_grad = halving_sum(kernel_part, ("space", "dp"), 3, riders=input_grad)
    kernel_grad = kernel_sum / pixel_count
    return (loss, input_grad.astype(jnp.bfloat16), kernel_grad, text_grad)


def solution(mesh):
    placed = (P("dp", "space", None, None), P(), P(), P(), P(), P(), P("dp", None), P())
    return jax.shard_map(
        shards,
        mesh=mesh,
        in_specs=placed,
        out_specs=(P(), P("dp", "space", None, None), P(), P("dp", None)),
        check_vma=False,
    )
```

```python
import jax
import jax.numpy as jnp
from jax import lax
from jax.experimental import pallas as pl
from jax.sharding import PartitionSpec as P


def with_halo(block, sides, width):
    for axis, dim in sides:
        count = lax.axis_size(axis)
        forward = [(i, i + 1) for i in range(count - 1)]
        backward = [(target, source) for source, target in forward]
        low = lax.ppermute(
            lax.slice_in_dim(block, block.shape[dim] - width, None, axis=dim), axis, forward
        )
        high = lax.ppermute(lax.slice_in_dim(block, 0, width, axis=dim), axis, backward)
        block = jnp.concatenate([low, block, high], axis=dim)
    return block


def butterfly_sum(values, axes, riders=None):
    riders_done = None
    for axis in axes:
        count = lax.axis_size(axis)
        if count & (count - 1):
            values = lax.psum(values, axis)
            continue
        step = 1
        while step < count:
            pairs = [(i, i ^ step) for i in range(count)]
            received = lax.ppermute(values, axis, pairs)
            if riders is not None:
                received, riders = lax.optimization_barrier((received, riders))
                riders_done = riders
                riders = None
            values = values + received
            step *= 2
    return values if riders_done is None else (values, riders_done)


def halving_sum(values, axes, split_steps, riders):
    steps = []
    for axis in axes:
        count = lax.axis_size(axis)
        if count & (count - 1):
            return butterfly_sum(values, axes)
        step = 1
        while step < count:
            steps.append((axis, count, step))
            step *= 2
    split_steps = min(split_steps, len(steps))
    riders_done = []
    parts = 1 << split_steps
    flat = values.reshape(-1)
    size = flat.shape[0]
    padded_size = -(-size // parts) * parts
    chunk = jnp.pad(flat, (0, padded_size - size))
    for axis, count, step in steps[:split_steps]:
        pairs = [(i, i ^ step) for i in range(count)]
        upper = (lax.axis_index(axis) // step) % 2 == 1
        half = chunk.shape[0] // 2
        low, high = chunk[:half], chunk[half:]
        keep = jnp.where(upper, high, low)
        give = jnp.where(upper, low, high)
        received = lax.ppermute(give, axis, pairs)
        if len(riders_done) < len(riders):
            received, rider = lax.optimization_barrier((received, riders[len(riders_done)]))
            riders_done.append(rider)
        chunk = keep + received
    for axis, count, step in steps[split_steps:]:
        pairs = [(i, i ^ step) for i in range(count)]
        chunk = chunk + lax.ppermute(chunk, axis, pairs)
    for axis, count, step in reversed(steps[:split_steps]):
        pairs = [(i, i ^ step) for i in range(count)]
        upper = (lax.axis_index(axis) // step) % 2 == 1
        other = lax.ppermute(chunk, axis, pairs)
        chunk = jnp.where(
            upper, jnp.concatenate([other, chunk]), jnp.concatenate([chunk, other])
        )
    return chunk[:size].reshape(values.shape), riders_done


def normalize(values):
    centre_value = jnp.mean(values, axis=-1, keepdims=True)
    centred = values - centre_value
    spread = jnp.mean(centred * centred, axis=-1, keepdims=True)
    inv_dev = lax.rsqrt(spread + 1e-06)
    return (centred * inv_dev, inv_dev)


def depthwise(extended, kernel, reach_cols, **options):
    channels = kernel.shape[-1]
    return lax.conv_general_dilated(
        extended,
        kernel.reshape(kernel.shape[0], kernel.shape[1], 1, channels),
        (1, 1),
        ((0, 0), (reach_cols, reach_cols)),
        dimension_numbers=("NHWC", "HWIO", "NHWC"),
        feature_group_count=channels,
        **options,
    )


def kernel_terms(grad_rows, padded, reach, lanes=128):
    row_count, col_count, channels = grad_rows.shape
    side = 2 * reach + 1
    groups = col_count // 8

    def body(g_ref, x_ref, o_ref):
        for a in range(side):
            for d in range(side):
                acc = jnp.zeros((8, lanes), jnp.float32)
                for h in range(row_count):
                    prod = g_ref[h] * x_ref[h + a, pl.ds(d, col_count), :]
                    acc = acc + prod.reshape(groups, 8, lanes).sum(axis=0)
                o_ref[a, pl.ds(d, 1), :] = acc.sum(axis=0, keepdims=True)

    return pl.pallas_call(
        body,
        grid=(channels // lanes,),
        in_specs=[
            pl.BlockSpec((row_count, col_count, lanes), lambda i: (0, 0, i)),
            pl.BlockSpec(padded.shape[:2] + (lanes,), lambda i: (0, 0, i)),
        ],
        out_specs=pl.BlockSpec((side, side, lanes), lambda i: (0, 0, i)),
        out_shape=jax.ShapeDtypeStruct((side, side, channels), jnp.float32),
    )(grad_rows, padded)

def input_terms(padded, kernel, row_count, first_block, block_count, lanes=128):
    side = kernel.shape[0]
    col_count = padded.shape[1] - side + 1
    channels = padded.shape[2]

    def body(x_ref, k_ref, o_ref):
        for h in range(row_count):
            acc = jnp.zeros((col_count, lanes), jnp.float32)
            for a in range(side):
                for d in range(side):
                    weight = k_ref[side - 1 - a, pl.ds(side - 1 - d, 1), :]
                    acc = acc + weight * x_ref[h + a, pl.ds(d, col_count), :]
            o_ref[h] = acc.astype(o_ref.dtype)

    return pl.pallas_call(
        body,
        grid=(block_count,),
        in_specs=[
            pl.BlockSpec(padded.shape[:2] + (lanes,), lambda i: (0, 0, i + first_block)),
            pl.BlockSpec((side, side, lanes), lambda i: (0, 0, i + first_block)),
        ],
        out_specs=pl.BlockSpec((row_count, col_count, lanes), lambda i: (0, 0, i)),
        out_shape=jax.ShapeDtypeStruct((row_count, col_count, block_count * lanes), jnp.bfloat16),
    )(padded, kernel)

def logsum(scores, axis):
    highest = jnp.max(scores, axis=axis, keepdims=True)
    return jnp.squeeze(highest, axis) + jnp.log(jnp.sum(jnp.exp(scores - highest), axis=axis))


def shards(images, dw_kernel, dw_bias, ln_gain, ln_shift, proj, text, logit_scale):
    batch_dev, row_count, col_count, channels = images.shape
    height = row_count * lax.axis_size("space")
    pixel_count = height * col_count
    batch_count = batch_dev * lax.axis_size("dp")
    reach_rows = dw_kernel.shape[0] // 2
    kernel_float = dw_kernel.astype(jnp.float32)
    extended = with_halo(images, (("space", 1),), reach_rows)
    padded_all = jnp.pad(
        extended.astype(jnp.float32), ((0, 0), (0, 0), (reach_rows, reach_rows), (0, 0))
    )
    conv_out = (
        depthwise(extended, dw_kernel, reach_rows, preferred_element_type=jnp.float32) + dw_bias
    )
    normed, inv_dev = normalize(conv_out)
    pool_part = jnp.sum(normed * ln_gain + ln_shift, axis=(1, 2))
    pool_sum, padded_all = butterfly_sum(pool_part, ("space",), riders=padded_all)
    first_row = lax.axis_index("dp") * batch_dev
    packed = jnp.concatenate([pool_sum, text], axis=1)
    table = lax.dynamic_update_slice(
        jnp.zeros((batch_count, packed.shape[1]), jnp.float32), packed, (first_row, 0)
    )
    table = butterfly_sum(table, ("dp",))
    pooled = table[:, :channels] / pixel_count
    all_text = table[:, channels:]
    proj_float = proj.astype(jnp.float32)
    embedded = jnp.dot(pooled, proj_float, precision=lax.Precision.HIGHEST)
    emb_norm = jnp.sqrt(jnp.sum(embedded * embedded, axis=-1, keepdims=True))
    unit_img = embedded / emb_norm
    text_norm = jnp.sqrt(jnp.sum(all_text * all_text, axis=-1, keepdims=True))
    unit_txt = all_text / text_norm
    factor = logit_scale[0]
    scores = factor * jnp.dot(unit_img, unit_txt.T, precision=lax.Precision.HIGHEST)
    row_logsum = logsum(scores, 1)
    col_logsum = logsum(scores, 0)
    identity = jnp.eye(batch_count, dtype=jnp.float32)
    diagonal = jnp.sum(scores * identity, axis=1)
    loss = (jnp.sum(row_logsum - diagonal) + jnp.sum(col_logsum - diagonal)) / (2 * batch_count)
    score_grad = (
        0.5
        * (
            jnp.exp(scores - row_logsum[:, None])
            + jnp.exp(scores - col_logsum[None, :])
        )
        - identity
    )
    unit_img_grad = factor * jnp.dot(score_grad, unit_txt, precision=lax.Precision.HIGHEST)
    unit_txt_grad = factor * jnp.dot(score_grad.T, unit_img, precision=lax.Precision.HIGHEST)
    text_grad_all = (
        unit_txt_grad - unit_txt * jnp.sum(unit_txt * unit_txt_grad, axis=-1, keepdims=True)
    ) / text_norm
    emb_grad_all = (
        unit_img_grad - unit_img * jnp.sum(unit_img * unit_img_grad, axis=-1, keepdims=True)
    ) / emb_norm
    text_grad = lax.dynamic_slice_in_dim(text_grad_all, first_row, batch_dev, axis=0)
    emb_grad = lax.dynamic_slice_in_dim(emb_grad_all, first_row, batch_dev, axis=0)
    weighted = jnp.dot(emb_grad, proj_float.T, precision=lax.Precision.HIGHEST) * ln_gain
    weight_rows = weighted[:, None, None, :]
    weight_mean = jnp.mean(weighted, axis=-1)[:, None, None, None]
    spread_term = jnp.mean(weight_rows * normed, axis=-1, keepdims=True)
    grad_own = inv_dev * (weight_rows - weight_mean - normed * spread_term)
    grad_wide = with_halo(grad_own, (("space", 1),), reach_rows)
    grad_pad = jnp.pad(grad_wide, ((0, 0), (0, 0), (reach_rows, reach_rows), (0, 0)))
    blocks = channels // 128
    halves = ((0, blocks // 2), (blocks // 2, blocks - blocks // 2))
    input_parts = [
        [input_terms(grad_pad[image], kernel_float, row_count, *half) for image in range(batch_dev)]
        for half in halves
    ]
    kernel_part = kernel_terms(grad_own[0], padded_all[0], reach_rows)
    for image in range(1, batch_dev):
        kernel_part = kernel_part + kernel_terms(grad_own[image], padded_all[image], reach_rows)
    kernel_sum, input_parts = halving_sum(kernel_part, ("space", "dp"), 3, input_parts)
    input_grad = jnp.stack(
        [jnp.concatenate([half[image] for half in input_parts], axis=-1) for image in range(batch_dev)]
    )
    kernel_grad = kernel_sum / pixel_count
    return (loss, input_grad.astype(jnp.bfloat16), kernel_grad, text_grad)


def solution(mesh):
    placed = (P("dp", "space", None, None), P(), P(), P(), P(), P(), P("dp", None), P())
    return jax.shard_map(
        shards,
        mesh=mesh,
        in_specs=placed,
        out_specs=(P(), P("dp", "space", None, None), P(), P("dp", None)),
        check_vma=False,
    )
```

```python
import jax
import jax.numpy as jnp
from jax import lax
from jax.experimental import pallas as pl
from jax.sharding import PartitionSpec as P


def with_halo(block, sides, width):
    for axis, dim in sides:
        count = lax.axis_size(axis)
        forward = [(i, i + 1) for i in range(count - 1)]
        backward = [(target, source) for source, target in forward]
        low = lax.ppermute(
            lax.slice_in_dim(block, block.shape[dim] - width, None, axis=dim), axis, forward
        )
        high = lax.ppermute(lax.slice_in_dim(block, 0, width, axis=dim), axis, backward)
        block = jnp.concatenate([low, block, high], axis=dim)
    return block


def butterfly_sum(values, axes, riders=None):
    riders_done = None
    for axis in axes:
        count = lax.axis_size(axis)
        if count & (count - 1):
            values = lax.psum(values, axis)
            continue
        step = 1
        while step < count:
            pairs = [(i, i ^ step) for i in range(count)]
            received = lax.ppermute(values, axis, pairs)
            if riders is not None:
                received, riders = lax.optimization_barrier((received, riders))
                riders_done = riders
                riders = None
            values = values + received
            step *= 2
    return values if riders_done is None else (values, riders_done)


def halving_sum(values, axes, split_steps, riders):
    steps = []
    for axis in axes:
        count = lax.axis_size(axis)
        if count & (count - 1):
            return butterfly_sum(values, axes)
        step = 1
        while step < count:
            steps.append((axis, count, step))
            step *= 2
    split_steps = min(split_steps, len(steps))
    riders_done = []
    parts = 1 << split_steps
    flat = values.reshape(-1)
    size = flat.shape[0]
    padded_size = -(-size // parts) * parts
    chunk = jnp.pad(flat, (0, padded_size - size))
    for axis, count, step in steps[:split_steps]:
        pairs = [(i, i ^ step) for i in range(count)]
        upper = (lax.axis_index(axis) // step) % 2 == 1
        half = chunk.shape[0] // 2
        low, high = chunk[:half], chunk[half:]
        keep = jnp.where(upper, high, low)
        give = jnp.where(upper, low, high)
        received = lax.ppermute(give, axis, pairs)
        if len(riders_done) < len(riders):
            rider = riders[len(riders_done)]
            if callable(rider):
                rider = rider(riders_done)
            received, rider = lax.optimization_barrier((received, rider))
            riders_done.append(rider)
        chunk = keep + received
    for axis, count, step in steps[split_steps:]:
        pairs = [(i, i ^ step) for i in range(count)]
        chunk = chunk + lax.ppermute(chunk, axis, pairs)
    for axis, count, step in reversed(steps[:split_steps]):
        pairs = [(i, i ^ step) for i in range(count)]
        upper = (lax.axis_index(axis) // step) % 2 == 1
        other = lax.ppermute(chunk, axis, pairs)
        chunk = jnp.where(
            upper, jnp.concatenate([other, chunk]), jnp.concatenate([chunk, other])
        )
    return chunk[:size].reshape(values.shape), riders_done


def normalize(values):
    centre_value = jnp.mean(values, axis=-1, keepdims=True)
    centred = values - centre_value
    spread = jnp.mean(centred * centred, axis=-1, keepdims=True)
    inv_dev = lax.rsqrt(spread + 1e-06)
    return (centred * inv_dev, inv_dev)


def depthwise(extended, kernel, reach_cols, **options):
    channels = kernel.shape[-1]
    return lax.conv_general_dilated(
        extended,
        kernel.reshape(kernel.shape[0], kernel.shape[1], 1, channels),
        (1, 1),
        ((0, 0), (reach_cols, reach_cols)),
        dimension_numbers=("NHWC", "HWIO", "NHWC"),
        feature_group_count=channels,
        **options,
    )


def kernel_terms(grad_rows, padded, reach, lanes=128):
    row_count, col_count, channels = grad_rows.shape
    side = 2 * reach + 1
    groups = col_count // 8

    def body(g_ref, x_ref, o_ref):
        for a in range(side):
            for d in range(side):
                acc = jnp.zeros((8, lanes), jnp.float32)
                for h in range(row_count):
                    prod = g_ref[h] * x_ref[h + a, pl.ds(d, col_count), :]
                    acc = acc + prod.reshape(groups, 8, lanes).sum(axis=0)
                o_ref[a, pl.ds(d, 1), :] = acc.sum(axis=0, keepdims=True)

    return pl.pallas_call(
        body,
        grid=(channels // lanes,),
        in_specs=[
            pl.BlockSpec((row_count, col_count, lanes), lambda i: (0, 0, i)),
            pl.BlockSpec(padded.shape[:2] + (lanes,), lambda i: (0, 0, i)),
        ],
        out_specs=pl.BlockSpec((side, side, lanes), lambda i: (0, 0, i)),
        out_shape=jax.ShapeDtypeStruct((side, side, channels), jnp.float32),
    )(grad_rows, padded)

def input_terms(padded, kernel, row_count, first_block, block_count, lanes=128):
    side = kernel.shape[0]
    col_count = padded.shape[1] - side + 1
    channels = padded.shape[2]

    def body(x_ref, k_ref, o_ref):
        for h in range(row_count):
            acc = jnp.zeros((col_count, lanes), jnp.float32)
            for a in range(side):
                for d in range(side):
                    weight = k_ref[side - 1 - a, pl.ds(side - 1 - d, 1), :]
                    acc = acc + weight * x_ref[h + a, pl.ds(d, col_count), :]
            o_ref[h] = acc.astype(o_ref.dtype)

    return pl.pallas_call(
        body,
        grid=(block_count,),
        in_specs=[
            pl.BlockSpec(padded.shape[:2] + (lanes,), lambda i: (0, 0, i + first_block)),
            pl.BlockSpec((side, side, lanes), lambda i: (0, 0, i + first_block)),
        ],
        out_specs=pl.BlockSpec((row_count, col_count, lanes), lambda i: (0, 0, i)),
        out_shape=jax.ShapeDtypeStruct((row_count, col_count, block_count * lanes), jnp.bfloat16),
    )(padded, kernel)

def logsum(scores, axis):
    highest = jnp.max(scores, axis=axis, keepdims=True)
    return jnp.squeeze(highest, axis) + jnp.log(jnp.sum(jnp.exp(scores - highest), axis=axis))


def shards(images, dw_kernel, dw_bias, ln_gain, ln_shift, proj, text, logit_scale):
    batch_dev, row_count, col_count, channels = images.shape
    height = row_count * lax.axis_size("space")
    pixel_count = height * col_count
    batch_count = batch_dev * lax.axis_size("dp")
    reach_rows = dw_kernel.shape[0] // 2
    kernel_float = dw_kernel.astype(jnp.float32)
    extended = with_halo(images, (("space", 1),), reach_rows)
    padded_all = jnp.pad(
        extended.astype(jnp.float32), ((0, 0), (0, 0), (reach_rows, reach_rows), (0, 0))
    )
    conv_out = (
        depthwise(extended, dw_kernel, reach_rows, preferred_element_type=jnp.float32) + dw_bias
    )
    normed, inv_dev = normalize(conv_out)
    pool_part = jnp.sum(normed * ln_gain + ln_shift, axis=(1, 2))
    pool_sum, padded_all = butterfly_sum(pool_part, ("space",), riders=padded_all)
    first_row = lax.axis_index("dp") * batch_dev
    packed = jnp.concatenate([pool_sum, text], axis=1)
    table = lax.dynamic_update_slice(
        jnp.zeros((batch_count, packed.shape[1]), jnp.float32), packed, (first_row, 0)
    )
    table = butterfly_sum(table, ("dp",))
    pooled = table[:, :channels] / pixel_count
    all_text = table[:, channels:]
    proj_float = proj.astype(jnp.float32)
    embedded = jnp.dot(pooled, proj_float, precision=lax.Precision.HIGHEST)
    emb_norm = jnp.sqrt(jnp.sum(embedded * embedded, axis=-1, keepdims=True))
    unit_img = embedded / emb_norm
    text_norm = jnp.sqrt(jnp.sum(all_text * all_text, axis=-1, keepdims=True))
    unit_txt = all_text / text_norm
    factor = logit_scale[0]
    scores = factor * jnp.dot(unit_img, unit_txt.T, precision=lax.Precision.HIGHEST)
    row_logsum = logsum(scores, 1)
    col_logsum = logsum(scores, 0)
    identity = jnp.eye(batch_count, dtype=jnp.float32)
    diagonal = jnp.sum(scores * identity, axis=1)
    loss = (jnp.sum(row_logsum - diagonal) + jnp.sum(col_logsum - diagonal)) / (2 * batch_count)
    score_grad = (
        0.5
        * (
            jnp.exp(scores - row_logsum[:, None])
            + jnp.exp(scores - col_logsum[None, :])
        )
        - identity
    )
    unit_img_grad = factor * jnp.dot(score_grad, unit_txt, precision=lax.Precision.HIGHEST)
    unit_txt_grad = factor * jnp.dot(score_grad.T, unit_img, precision=lax.Precision.HIGHEST)
    text_grad_all = (
        unit_txt_grad - unit_txt * jnp.sum(unit_txt * unit_txt_grad, axis=-1, keepdims=True)
    ) / text_norm
    emb_grad_all = (
        unit_img_grad - unit_img * jnp.sum(unit_img * unit_img_grad, axis=-1, keepdims=True)
    ) / emb_norm
    text_grad = lax.dynamic_slice_in_dim(text_grad_all, first_row, batch_dev, axis=0)
    emb_grad = lax.dynamic_slice_in_dim(emb_grad_all, first_row, batch_dev, axis=0)
    weighted = jnp.dot(emb_grad, proj_float.T, precision=lax.Precision.HIGHEST) * ln_gain
    weight_rows = weighted[:, None, None, :]
    weight_mean = jnp.mean(weighted, axis=-1)[:, None, None, None]
    spread_term = jnp.mean(weight_rows * normed, axis=-1, keepdims=True)
    grad_own = inv_dev * (weight_rows - weight_mean - normed * spread_term)
    grad_wide = with_halo(grad_own, (("space", 1),), reach_rows)
    grad_pad = jnp.pad(grad_wide, ((0, 0), (0, 0), (reach_rows, reach_rows), (0, 0)))
    blocks = channels // 128
    halves = ((0, blocks // 2), (blocks // 2, blocks - blocks // 2))
    input_parts = [
        [input_terms(grad_pad[image], kernel_float, row_count, *half) for image in range(batch_dev)]
        for half in halves
    ]
    kernel_part = kernel_terms(grad_own[0], padded_all[0], reach_rows)
    for image in range(1, batch_dev):
        kernel_part = kernel_part + kernel_terms(grad_own[image], padded_all[image], reach_rows)
    def join(done):
        return jnp.stack(
            [jnp.concatenate([half[image] for half in done], axis=-1) for image in range(batch_dev)]
        )

    kernel_sum, riders_done = halving_sum(
        kernel_part, ("space", "dp"), 3, input_parts + [join]
    )
    input_grad = riders_done[-1]
    kernel_grad = kernel_sum / pixel_count
    return (loss, input_grad.astype(jnp.bfloat16), kernel_grad, text_grad)


def solution(mesh):
    placed = (P("dp", "space", None, None), P(), P(), P(), P(), P(), P("dp", None), P())
    return jax.shard_map(
        shards,
        mesh=mesh,
        in_specs=placed,
        out_specs=(P(), P("dp", "space", None, None), P(), P("dp", None)),
        check_vma=False,
    )
```

```python
import jax
import jax.numpy as jnp
from jax import lax
from jax.experimental import pallas as pl
from jax.sharding import PartitionSpec as P


def with_halo(block, sides, width):
    for axis, dim in sides:
        count = lax.axis_size(axis)
        forward = [(i, i + 1) for i in range(count - 1)]
        backward = [(target, source) for source, target in forward]
        low = lax.ppermute(
            lax.slice_in_dim(block, block.shape[dim] - width, None, axis=dim), axis, forward
        )
        high = lax.ppermute(lax.slice_in_dim(block, 0, width, axis=dim), axis, backward)
        block = jnp.concatenate([low, block, high], axis=dim)
    return block


def butterfly_sum(values, axes, riders=None):
    riders_done = None
    for axis in axes:
        count = lax.axis_size(axis)
        if count & (count - 1):
            values = lax.psum(values, axis)
            continue
        step = 1
        while step < count:
            pairs = [(i, i ^ step) for i in range(count)]
            received = lax.ppermute(values, axis, pairs)
            if riders is not None:
                received, riders = lax.optimization_barrier((received, riders))
                riders_done = riders
                riders = None
            values = values + received
            step *= 2
    return values if riders_done is None else (values, riders_done)


def halving_sum(values, axes, split_steps, riders):
    steps = []
    for axis in axes:
        count = lax.axis_size(axis)
        if count & (count - 1):
            return butterfly_sum(values, axes)
        step = 1
        while step < count:
            steps.append((axis, count, step))
            step *= 2
    split_steps = min(split_steps, len(steps))
    riders_done = []
    parts = 1 << split_steps
    flat = values.reshape(-1)
    size = flat.shape[0]
    padded_size = -(-size // parts) * parts
    chunk = jnp.pad(flat, (0, padded_size - size))
    for axis, count, step in steps[:split_steps]:
        pairs = [(i, i ^ step) for i in range(count)]
        upper = (lax.axis_index(axis) // step) % 2 == 1
        half = chunk.shape[0] // 2
        low, high = chunk[:half], chunk[half:]
        keep = jnp.where(upper, high, low)
        give = jnp.where(upper, low, high)
        received = lax.ppermute(give, axis, pairs)
        if len(riders_done) < len(riders):
            received, rider = lax.optimization_barrier((received, riders[len(riders_done)]))
            riders_done.append(rider)
        chunk = keep + received
    for axis, count, step in steps[split_steps:]:
        pairs = [(i, i ^ step) for i in range(count)]
        chunk = chunk + lax.ppermute(chunk, axis, pairs)
    for axis, count, step in reversed(steps[:split_steps]):
        pairs = [(i, i ^ step) for i in range(count)]
        upper = (lax.axis_index(axis) // step) % 2 == 1
        other = lax.ppermute(chunk, axis, pairs)
        chunk = jnp.where(
            upper, jnp.concatenate([other, chunk]), jnp.concatenate([chunk, other])
        )
    return chunk[:size].reshape(values.shape), riders_done


def normalize(values):
    centre_value = jnp.mean(values, axis=-1, keepdims=True)
    centred = values - centre_value
    spread = jnp.mean(centred * centred, axis=-1, keepdims=True)
    inv_dev = lax.rsqrt(spread + 1e-06)
    return (centred * inv_dev, inv_dev)


def depthwise(extended, kernel, reach_cols, **options):
    channels = kernel.shape[-1]
    return lax.conv_general_dilated(
        extended,
        kernel.reshape(kernel.shape[0], kernel.shape[1], 1, channels),
        (1, 1),
        ((0, 0), (reach_cols, reach_cols)),
        dimension_numbers=("NHWC", "HWIO", "NHWC"),
        feature_group_count=channels,
        **options,
    )


def kernel_terms(grad_rows, padded, reach, scale, lanes=128):
    row_count, col_count, channels = grad_rows.shape
    side = 2 * reach + 1
    groups = col_count // 8

    def body(g_ref, x_ref, o_ref):
        for a in range(side):
            for d in range(side):
                acc = jnp.zeros((8, lanes), jnp.float32)
                for h in range(row_count):
                    prod = g_ref[h] * x_ref[h + a, pl.ds(d, col_count), :]
                    acc = acc + prod.reshape(groups, 8, lanes).sum(axis=0)
                o_ref[a, pl.ds(d, 1), :] = acc.sum(axis=0, keepdims=True) * scale

    return pl.pallas_call(
        body,
        grid=(channels // lanes,),
        in_specs=[
            pl.BlockSpec((row_count, col_count, lanes), lambda i: (0, 0, i)),
            pl.BlockSpec(padded.shape[:2] + (lanes,), lambda i: (0, 0, i)),
        ],
        out_specs=pl.BlockSpec((side, side, lanes), lambda i: (0, 0, i)),
        out_shape=jax.ShapeDtypeStruct((side, side, channels), jnp.float32),
    )(grad_rows, padded)

def input_terms(padded, kernel, row_count, first_block, block_count, lanes=128):
    side = kernel.shape[0]
    col_count = padded.shape[1] - side + 1
    channels = padded.shape[2]

    def body(x_ref, k_ref, o_ref):
        for h in range(row_count):
            acc = jnp.zeros((col_count, lanes), jnp.float32)
            for a in range(side):
                for d in range(side):
                    weight = k_ref[side - 1 - a, pl.ds(side - 1 - d, 1), :]
                    acc = acc + weight * x_ref[h + a, pl.ds(d, col_count), :]
            o_ref[h] = acc.astype(o_ref.dtype)

    return pl.pallas_call(
        body,
        grid=(block_count,),
        in_specs=[
            pl.BlockSpec(padded.shape[:2] + (lanes,), lambda i: (0, 0, i + first_block)),
            pl.BlockSpec((side, side, lanes), lambda i: (0, 0, i + first_block)),
        ],
        out_specs=pl.BlockSpec((row_count, col_count, lanes), lambda i: (0, 0, i)),
        out_shape=jax.ShapeDtypeStruct((row_count, col_count, block_count * lanes), jnp.bfloat16),
    )(padded, kernel)

def logsum(scores, axis):
    highest = jnp.max(scores, axis=axis, keepdims=True)
    return jnp.squeeze(highest, axis) + jnp.log(jnp.sum(jnp.exp(scores - highest), axis=axis))


def shards(images, dw_kernel, dw_bias, ln_gain, ln_shift, proj, text, logit_scale):
    batch_dev, row_count, col_count, channels = images.shape
    height = row_count * lax.axis_size("space")
    pixel_count = height * col_count
    batch_count = batch_dev * lax.axis_size("dp")
    reach_rows = dw_kernel.shape[0] // 2
    kernel_float = dw_kernel.astype(jnp.float32)
    extended = with_halo(images, (("space", 1),), reach_rows)
    padded_all = jnp.pad(
        extended.astype(jnp.float32), ((0, 0), (0, 0), (reach_rows, reach_rows), (0, 0))
    )
    conv_out = (
        depthwise(extended, dw_kernel, reach_rows, preferred_element_type=jnp.float32) + dw_bias
    )
    normed, inv_dev = normalize(conv_out)
    pool_part = jnp.sum(normed * ln_gain + ln_shift, axis=(1, 2))
    pool_sum, padded_all = butterfly_sum(pool_part, ("space",), riders=padded_all)
    first_row = lax.axis_index("dp") * batch_dev
    packed = jnp.concatenate([pool_sum, text], axis=1)
    table = lax.dynamic_update_slice(
        jnp.zeros((batch_count, packed.shape[1]), jnp.float32), packed, (first_row, 0)
    )
    table = butterfly_sum(table, ("dp",))
    pooled = table[:, :channels] / pixel_count
    all_text = table[:, channels:]
    proj_float = proj.astype(jnp.float32)
    embedded = jnp.dot(pooled, proj_float, precision=lax.Precision.HIGHEST)
    emb_norm = jnp.sqrt(jnp.sum(embedded * embedded, axis=-1, keepdims=True))
    unit_img = embedded / emb_norm
    text_norm = jnp.sqrt(jnp.sum(all_text * all_text, axis=-1, keepdims=True))
    unit_txt = all_text / text_norm
    factor = logit_scale[0]
    scores = factor * jnp.dot(unit_img, unit_txt.T, precision=lax.Precision.HIGHEST)
    row_logsum = logsum(scores, 1)
    col_logsum = logsum(scores, 0)
    identity = jnp.eye(batch_count, dtype=jnp.float32)
    diagonal = jnp.sum(scores * identity, axis=1)
    loss = (jnp.sum(row_logsum - diagonal) + jnp.sum(col_logsum - diagonal)) / (2 * batch_count)
    score_grad = (
        0.5
        * (
            jnp.exp(scores - row_logsum[:, None])
            + jnp.exp(scores - col_logsum[None, :])
        )
        - identity
    )
    unit_img_grad = factor * jnp.dot(score_grad, unit_txt, precision=lax.Precision.HIGHEST)
    unit_txt_grad = factor * jnp.dot(score_grad.T, unit_img, precision=lax.Precision.HIGHEST)
    text_grad_all = (
        unit_txt_grad - unit_txt * jnp.sum(unit_txt * unit_txt_grad, axis=-1, keepdims=True)
    ) / text_norm
    emb_grad_all = (
        unit_img_grad - unit_img * jnp.sum(unit_img * unit_img_grad, axis=-1, keepdims=True)
    ) / emb_norm
    text_grad = lax.dynamic_slice_in_dim(text_grad_all, first_row, batch_dev, axis=0)
    emb_grad = lax.dynamic_slice_in_dim(emb_grad_all, first_row, batch_dev, axis=0)
    weighted = jnp.dot(emb_grad, proj_float.T, precision=lax.Precision.HIGHEST) * ln_gain
    weight_rows = weighted[:, None, None, :]
    weight_mean = jnp.mean(weighted, axis=-1)[:, None, None, None]
    spread_term = jnp.mean(weight_rows * normed, axis=-1, keepdims=True)
    grad_own = inv_dev * (weight_rows - weight_mean - normed * spread_term)
    grad_wide = with_halo(grad_own, (("space", 1),), reach_rows)
    grad_pad = jnp.pad(grad_wide, ((0, 0), (0, 0), (reach_rows, reach_rows), (0, 0)))
    blocks = channels // 128
    halves = ((0, blocks // 2), (blocks // 2, blocks - blocks // 2))
    input_parts = [
        [input_terms(grad_pad[image], kernel_float, row_count, *half) for image in range(batch_dev)]
        for half in halves
    ]
    kernel_part = kernel_terms(grad_own[0], padded_all[0], reach_rows, 1.0 / pixel_count)
    for image in range(1, batch_dev):
        kernel_part = kernel_part + kernel_terms(
            grad_own[image], padded_all[image], reach_rows, 1.0 / pixel_count
        )
    kernel_grad, riders_done = halving_sum(
        kernel_part, ("space", "dp"), 3, input_parts + [text_grad]
    )
    input_parts, text_grad = riders_done[:2], riders_done[2]
    input_grad = jnp.stack(
        [jnp.concatenate([half[image] for half in input_parts], axis=-1) for image in range(batch_dev)]
    )
    return (loss, input_grad.astype(jnp.bfloat16), kernel_grad, text_grad)


def solution(mesh):
    placed = (P("dp", "space", None, None), P(), P(), P(), P(), P(), P("dp", None), P())
    return jax.shard_map(
        shards,
        mesh=mesh,
        in_specs=placed,
        out_specs=(P(), P("dp", "space", None, None), P(), P("dp", None)),
        check_vma=False,
    )
```

```python
import jax
import jax.numpy as jnp
from jax import lax
from jax.experimental import pallas as pl
from jax.sharding import PartitionSpec as P


def with_halo(block, sides, width):
    for axis, dim in sides:
        count = lax.axis_size(axis)
        forward = [(i, i + 1) for i in range(count - 1)]
        backward = [(target, source) for source, target in forward]
        low = lax.ppermute(
            lax.slice_in_dim(block, block.shape[dim] - width, None, axis=dim), axis, forward
        )
        high = lax.ppermute(lax.slice_in_dim(block, 0, width, axis=dim), axis, backward)
        block = jnp.concatenate([low, block, high], axis=dim)
    return block


def butterfly_sum(values, axes, riders=None):
    riders_done = None
    for axis in axes:
        count = lax.axis_size(axis)
        if count & (count - 1):
            values = lax.psum(values, axis)
            continue
        step = 1
        while step < count:
            pairs = [(i, i ^ step) for i in range(count)]
            received = lax.ppermute(values, axis, pairs)
            if riders is not None:
                received, riders = lax.optimization_barrier((received, riders))
                riders_done = riders
                riders = None
            values = values + received
            step *= 2
    return values if riders_done is None else (values, riders_done)


def halving_sum(values, axes, split_steps, riders):
    steps = []
    for axis in axes:
        count = lax.axis_size(axis)
        if count & (count - 1):
            return butterfly_sum(values, axes)
        step = 1
        while step < count:
            steps.append((axis, count, step))
            step *= 2
    split_steps = min(split_steps, len(steps))
    riders_done = []
    parts = 1 << split_steps
    flat = values.reshape(-1)
    size = flat.shape[0]
    padded_size = -(-size // parts) * parts
    chunk = jnp.pad(flat, (0, padded_size - size))
    for axis, count, step in steps[:split_steps]:
        pairs = [(i, i ^ step) for i in range(count)]
        upper = (lax.axis_index(axis) // step) % 2 == 1
        half = chunk.shape[0] // 2
        low, high = chunk[:half], chunk[half:]
        keep = jnp.where(upper, high, low)
        give = jnp.where(upper, low, high)
        received = lax.ppermute(give, axis, pairs)
        if len(riders_done) < len(riders):
            received, rider = lax.optimization_barrier((received, riders[len(riders_done)]))
            riders_done.append(rider)
        chunk = keep + received
    for axis, count, step in steps[split_steps:]:
        pairs = [(i, i ^ step) for i in range(count)]
        chunk = chunk + lax.ppermute(chunk, axis, pairs)
    for axis, count, step in reversed(steps[:split_steps]):
        pairs = [(i, i ^ step) for i in range(count)]
        upper = (lax.axis_index(axis) // step) % 2 == 1
        other = lax.ppermute(chunk, axis, pairs)
        chunk = jnp.where(
            upper, jnp.concatenate([other, chunk]), jnp.concatenate([chunk, other])
        )
    return chunk[:size].reshape(values.shape), riders_done


def normalize(values):
    centre_value = jnp.mean(values, axis=-1, keepdims=True)
    centred = values - centre_value
    spread = jnp.mean(centred * centred, axis=-1, keepdims=True)
    inv_dev = lax.rsqrt(spread + 1e-06)
    return (centred * inv_dev, inv_dev)


def depthwise(extended, kernel, reach_cols, **options):
    channels = kernel.shape[-1]
    return lax.conv_general_dilated(
        extended,
        kernel.reshape(kernel.shape[0], kernel.shape[1], 1, channels),
        (1, 1),
        ((0, 0), (reach_cols, reach_cols)),
        dimension_numbers=("NHWC", "HWIO", "NHWC"),
        feature_group_count=channels,
        **options,
    )


def kernel_terms(grad_rows, padded, reach, lanes=128):
    row_count, col_count, channels = grad_rows.shape
    side = 2 * reach + 1
    groups = col_count // 8

    def body(g_ref, x_ref, o_ref):
        for a in range(side):
            for d in range(side):
                acc = jnp.zeros((8, lanes), jnp.float32)
                for h in range(row_count):
                    prod = g_ref[h] * x_ref[h + a, pl.ds(d, col_count), :]
                    acc = acc + prod.reshape(groups, 8, lanes).sum(axis=0)
                o_ref[a, pl.ds(d, 1), :] = acc.sum(axis=0, keepdims=True)

    return pl.pallas_call(
        body,
        grid=(channels // lanes,),
        in_specs=[
            pl.BlockSpec((row_count, col_count, lanes), lambda i: (0, 0, i)),
            pl.BlockSpec(padded.shape[:2] + (lanes,), lambda i: (0, 0, i)),
        ],
        out_specs=pl.BlockSpec((side, side, lanes), lambda i: (0, 0, i)),
        out_shape=jax.ShapeDtypeStruct((side, side, channels), jnp.float32),
    )(grad_rows, padded)

def input_terms(padded, kernel, row_count, first_block, block_count, lanes=128):
    side = kernel.shape[0]
    col_count = padded.shape[1] - side + 1
    channels = padded.shape[2]

    def body(x_ref, k_ref, o_ref):
        for h in range(row_count):
            acc = jnp.zeros((col_count, lanes), jnp.float32)
            for a in range(side):
                for d in range(side):
                    weight = k_ref[side - 1 - a, pl.ds(side - 1 - d, 1), :]
                    acc = acc + weight * x_ref[h + a, pl.ds(d, col_count), :]
            o_ref[h] = acc.astype(o_ref.dtype)

    return pl.pallas_call(
        body,
        grid=(block_count,),
        in_specs=[
            pl.BlockSpec(padded.shape[:2] + (lanes,), lambda i: (0, 0, i + first_block)),
            pl.BlockSpec((side, side, lanes), lambda i: (0, 0, i + first_block)),
        ],
        out_specs=pl.BlockSpec((row_count, col_count, lanes), lambda i: (0, 0, i)),
        out_shape=jax.ShapeDtypeStruct((row_count, col_count, block_count * lanes), jnp.bfloat16),
    )(padded, kernel)

def logsum(scores, axis):
    highest = jnp.max(scores, axis=axis, keepdims=True)
    return jnp.squeeze(highest, axis) + jnp.log(jnp.sum(jnp.exp(scores - highest), axis=axis))


def shards(images, dw_kernel, dw_bias, ln_gain, ln_shift, proj, text, logit_scale):
    batch_dev, row_count, col_count, channels = images.shape
    height = row_count * lax.axis_size("space")
    pixel_count = height * col_count
    batch_count = batch_dev * lax.axis_size("dp")
    reach_rows = dw_kernel.shape[0] // 2
    kernel_float = dw_kernel.astype(jnp.float32)
    extended = with_halo(images, (("space", 1),), reach_rows)
    padded_all = jnp.pad(
        extended.astype(jnp.float32), ((0, 0), (0, 0), (reach_rows, reach_rows), (0, 0))
    )
    conv_out = (
        depthwise(extended, dw_kernel, reach_rows, preferred_element_type=jnp.float32) + dw_bias
    )
    normed, inv_dev = normalize(conv_out)
    pool_part = jnp.sum(normed * ln_gain + ln_shift, axis=(1, 2))
    pool_sum, padded_all = butterfly_sum(pool_part, ("space",), riders=padded_all)
    first_row = lax.axis_index("dp") * batch_dev
    packed = jnp.concatenate([pool_sum, text], axis=1)
    table = lax.dynamic_update_slice(
        jnp.zeros((batch_count, packed.shape[1]), jnp.float32), packed, (first_row, 0)
    )
    table = butterfly_sum(table, ("dp",))
    pooled = table[:, :channels] / pixel_count
    all_text = table[:, channels:]
    proj_float = proj.astype(jnp.float32)
    embedded = jnp.dot(pooled, proj_float, precision=lax.Precision.HIGHEST)
    emb_norm = jnp.sqrt(jnp.sum(embedded * embedded, axis=-1, keepdims=True))
    unit_img = embedded / emb_norm
    text_norm = jnp.sqrt(jnp.sum(all_text * all_text, axis=-1, keepdims=True))
    unit_txt = all_text / text_norm
    factor = logit_scale[0]
    scores = factor * jnp.dot(unit_img, unit_txt.T, precision=lax.Precision.HIGHEST)
    row_logsum = logsum(scores, 1)
    col_logsum = logsum(scores, 0)
    identity = jnp.eye(batch_count, dtype=jnp.float32)
    diagonal = jnp.sum(scores * identity, axis=1)
    loss = (jnp.sum(row_logsum - diagonal) + jnp.sum(col_logsum - diagonal)) / (2 * batch_count)
    score_grad = (
        0.5
        * (
            jnp.exp(scores - row_logsum[:, None])
            + jnp.exp(scores - col_logsum[None, :])
        )
        - identity
    )
    unit_img_grad = factor * jnp.dot(score_grad, unit_txt, precision=lax.Precision.HIGHEST)
    unit_txt_grad = factor * jnp.dot(score_grad.T, unit_img, precision=lax.Precision.HIGHEST)
    text_grad_all = (
        unit_txt_grad - unit_txt * jnp.sum(unit_txt * unit_txt_grad, axis=-1, keepdims=True)
    ) / text_norm
    emb_grad_all = (
        unit_img_grad - unit_img * jnp.sum(unit_img * unit_img_grad, axis=-1, keepdims=True)
    ) / emb_norm
    text_grad = lax.dynamic_slice_in_dim(text_grad_all, first_row, batch_dev, axis=0)
    emb_grad = lax.dynamic_slice_in_dim(emb_grad_all, first_row, batch_dev, axis=0)
    weighted = jnp.dot(emb_grad, proj_float.T, precision=lax.Precision.HIGHEST) * ln_gain
    weight_rows = weighted[:, None, None, :]
    weight_mean = jnp.mean(weighted, axis=-1)[:, None, None, None]
    spread_term = jnp.mean(weight_rows * normed, axis=-1, keepdims=True)
    grad_own = inv_dev * (weight_rows - weight_mean - normed * spread_term)
    grad_wide = with_halo(grad_own, (("space", 1),), reach_rows)
    grad_pad = jnp.pad(grad_wide, ((0, 0), (0, 0), (reach_rows, reach_rows), (0, 0)))
    blocks = channels // 128
    cuts = [blocks * k // 3 for k in range(4)]
    halves = [(cuts[k], cuts[k + 1] - cuts[k]) for k in range(3)]
    input_parts = [
        [input_terms(grad_pad[image], kernel_float, row_count, *half) for image in range(batch_dev)]
        for half in halves
    ]
    kernel_part = kernel_terms(grad_own[0], padded_all[0], reach_rows)
    for image in range(1, batch_dev):
        kernel_part = kernel_part + kernel_terms(grad_own[image], padded_all[image], reach_rows)
    kernel_sum, input_parts = halving_sum(kernel_part, ("space", "dp"), 3, input_parts)
    input_grad = jnp.stack(
        [jnp.concatenate([half[image] for half in input_parts], axis=-1) for image in range(batch_dev)]
    )
    kernel_grad = kernel_sum / pixel_count
    return (loss, input_grad.astype(jnp.bfloat16), kernel_grad, text_grad)


def solution(mesh):
    placed = (P("dp", "space", None, None), P(), P(), P(), P(), P(), P("dp", None), P())
    return jax.shard_map(
        shards,
        mesh=mesh,
        in_specs=placed,
        out_specs=(P(), P("dp", "space", None, None), P(), P("dp", None)),
        check_vma=False,
    )
```

```python
import jax
import jax.numpy as jnp
from jax import lax
from jax.experimental import pallas as pl
from jax.sharding import PartitionSpec as P


def with_halo(block, sides, width):
    for axis, dim in sides:
        count = lax.axis_size(axis)
        forward = [(i, i + 1) for i in range(count - 1)]
        backward = [(target, source) for source, target in forward]
        low = lax.ppermute(
            lax.slice_in_dim(block, block.shape[dim] - width, None, axis=dim), axis, forward
        )
        high = lax.ppermute(lax.slice_in_dim(block, 0, width, axis=dim), axis, backward)
        block = jnp.concatenate([low, block, high], axis=dim)
    return block


def butterfly_sum(values, axes, riders=None):
    riders_done = None
    for axis in axes:
        count = lax.axis_size(axis)
        if count & (count - 1):
            values = lax.psum(values, axis)
            continue
        step = 1
        while step < count:
            pairs = [(i, i ^ step) for i in range(count)]
            received = lax.ppermute(values, axis, pairs)
            if riders is not None:
                received, riders = lax.optimization_barrier((received, riders))
                riders_done = riders
                riders = None
            values = values + received
            step *= 2
    return values if riders_done is None else (values, riders_done)


def halving_sum(values, axes, split_steps, riders):
    steps = []
    for axis in axes:
        count = lax.axis_size(axis)
        if count & (count - 1):
            return butterfly_sum(values, axes)
        step = 1
        while step < count:
            steps.append((axis, count, step))
            step *= 2
    split_steps = min(split_steps, len(steps))
    riders_done = []
    parts = 1 << split_steps
    flat = values.reshape(-1)
    size = flat.shape[0]
    padded_size = -(-size // parts) * parts
    chunk = jnp.pad(flat, (0, padded_size - size))
    for axis, count, step in steps[:split_steps]:
        pairs = [(i, i ^ step) for i in range(count)]
        upper = (lax.axis_index(axis) // step) % 2 == 1
        half = chunk.shape[0] // 2
        low, high = chunk[:half], chunk[half:]
        keep = jnp.where(upper, high, low)
        give = jnp.where(upper, low, high)
        received = lax.ppermute(give, axis, pairs)
        if len(riders_done) < len(riders):
            received, rider = lax.optimization_barrier((received, riders[len(riders_done)]))
            riders_done.append(rider)
        chunk = keep + received
    for axis, count, step in steps[split_steps:]:
        pairs = [(i, i ^ step) for i in range(count)]
        chunk = chunk + lax.ppermute(chunk, axis, pairs)
    for axis, count, step in reversed(steps[:split_steps]):
        pairs = [(i, i ^ step) for i in range(count)]
        upper = (lax.axis_index(axis) // step) % 2 == 1
        other = lax.ppermute(chunk, axis, pairs)
        chunk = jnp.where(
            upper, jnp.concatenate([other, chunk]), jnp.concatenate([chunk, other])
        )
    return chunk[:size].reshape(values.shape), riders_done


def normalize(values):
    centre_value = jnp.mean(values, axis=-1, keepdims=True)
    centred = values - centre_value
    spread = jnp.mean(centred * centred, axis=-1, keepdims=True)
    inv_dev = lax.rsqrt(spread + 1e-06)
    return (centred * inv_dev, inv_dev)


def depthwise(extended, kernel, reach_cols, **options):
    channels = kernel.shape[-1]
    return lax.conv_general_dilated(
        extended,
        kernel.reshape(kernel.shape[0], kernel.shape[1], 1, channels),
        (1, 1),
        ((0, 0), (reach_cols, reach_cols)),
        dimension_numbers=("NHWC", "HWIO", "NHWC"),
        feature_group_count=channels,
        **options,
    )


def kernel_terms(grad_rows, padded, reach, lanes=128):
    row_count, col_count, channels = grad_rows.shape
    side = 2 * reach + 1
    groups = col_count // 8

    def body(g_ref, x_ref, o_ref):
        for a in range(side):
            for d in range(side):
                acc = jnp.zeros((8, lanes), jnp.float32)
                for h in range(row_count):
                    prod = g_ref[h] * x_ref[h + a, pl.ds(d, col_count), :]
                    acc = acc + prod.reshape(groups, 8, lanes).sum(axis=0)
                o_ref[a, pl.ds(d, 1), :] = acc.sum(axis=0, keepdims=True)

    return pl.pallas_call(
        body,
        grid=(channels // lanes,),
        in_specs=[
            pl.BlockSpec((row_count, col_count, lanes), lambda i: (0, 0, i)),
            pl.BlockSpec(padded.shape[:2] + (lanes,), lambda i: (0, 0, i)),
        ],
        out_specs=pl.BlockSpec((side, side, lanes), lambda i: (0, 0, i)),
        out_shape=jax.ShapeDtypeStruct((side, side, channels), jnp.float32),
    )(grad_rows, padded)

def input_terms(padded, kernel, row_count, first_block, block_count, lanes=128):
    side = kernel.shape[0]
    col_count = padded.shape[1] - side + 1
    channels = padded.shape[2]

    def body(x_ref, k_ref, o_ref):
        for h in range(row_count):
            acc = jnp.zeros((col_count, lanes), jnp.float32)
            for a in range(side):
                for d in range(side):
                    weight = k_ref[side - 1 - a, pl.ds(side - 1 - d, 1), :]
                    acc = acc + weight * x_ref[h + a, pl.ds(d, col_count), :]
            o_ref[h] = acc.astype(o_ref.dtype)

    return pl.pallas_call(
        body,
        grid=(block_count,),
        in_specs=[
            pl.BlockSpec(padded.shape[:2] + (lanes,), lambda i: (0, 0, i + first_block)),
            pl.BlockSpec((side, side, lanes), lambda i: (0, 0, i + first_block)),
        ],
        out_specs=pl.BlockSpec((row_count, col_count, lanes), lambda i: (0, 0, i)),
        out_shape=jax.ShapeDtypeStruct((row_count, col_count, block_count * lanes), jnp.bfloat16),
    )(padded, kernel)

def dot_exact(values, weights, contract):
    high = lax.reduce_precision(values, exponent_bits=8, mantissa_bits=7)
    rest = values - high
    middle = lax.reduce_precision(rest, exponent_bits=8, mantissa_bits=7)
    low = rest - middle
    dims = (((1,), (contract,)), ((), ()))
    parts = [
        lax.dot_general(
            part.astype(jnp.bfloat16), weights, dims, preferred_element_type=jnp.float32
        )
        for part in (high, middle, low)
    ]
    return parts[0] + (parts[1] + parts[2])


def logsum(scores, axis):
    highest = jnp.max(scores, axis=axis, keepdims=True)
    return jnp.squeeze(highest, axis) + jnp.log(jnp.sum(jnp.exp(scores - highest), axis=axis))


def shards(images, dw_kernel, dw_bias, ln_gain, ln_shift, proj, text, logit_scale):
    batch_dev, row_count, col_count, channels = images.shape
    height = row_count * lax.axis_size("space")
    pixel_count = height * col_count
    batch_count = batch_dev * lax.axis_size("dp")
    reach_rows = dw_kernel.shape[0] // 2
    kernel_float = dw_kernel.astype(jnp.float32)
    extended = with_halo(images, (("space", 1),), reach_rows)
    padded_all = jnp.pad(
        extended.astype(jnp.float32), ((0, 0), (0, 0), (reach_rows, reach_rows), (0, 0))
    )
    conv_out = (
        depthwise(extended, dw_kernel, reach_rows, preferred_element_type=jnp.float32) + dw_bias
    )
    normed, inv_dev = normalize(conv_out)
    pool_part = jnp.sum(normed * ln_gain + ln_shift, axis=(1, 2))
    pool_sum, padded_all = butterfly_sum(pool_part, ("space",), riders=padded_all)
    first_row = lax.axis_index("dp") * batch_dev
    packed = jnp.concatenate([pool_sum, text], axis=1)
    table = lax.dynamic_update_slice(
        jnp.zeros((batch_count, packed.shape[1]), jnp.float32), packed, (first_row, 0)
    )
    table = butterfly_sum(table, ("dp",))
    pooled = table[:, :channels] / pixel_count
    all_text = table[:, channels:]
    embedded = dot_exact(pooled, proj, 0)
    emb_norm = jnp.sqrt(jnp.sum(embedded * embedded, axis=-1, keepdims=True))
    unit_img = embedded / emb_norm
    text_norm = jnp.sqrt(jnp.sum(all_text * all_text, axis=-1, keepdims=True))
    unit_txt = all_text / text_norm
    factor = logit_scale[0]
    scores = factor * jnp.dot(unit_img, unit_txt.T, precision=lax.Precision.HIGHEST)
    row_logsum = logsum(scores, 1)
    col_logsum = logsum(scores, 0)
    identity = jnp.eye(batch_count, dtype=jnp.float32)
    diagonal = jnp.sum(scores * identity, axis=1)
    loss = (jnp.sum(row_logsum - diagonal) + jnp.sum(col_logsum - diagonal)) / (2 * batch_count)
    score_grad = (
        0.5
        * (
            jnp.exp(scores - row_logsum[:, None])
            + jnp.exp(scores - col_logsum[None, :])
        )
        - identity
    )
    unit_img_grad = factor * jnp.dot(score_grad, unit_txt, precision=lax.Precision.HIGHEST)
    unit_txt_grad = factor * jnp.dot(score_grad.T, unit_img, precision=lax.Precision.HIGHEST)
    text_grad_all = (
        unit_txt_grad - unit_txt * jnp.sum(unit_txt * unit_txt_grad, axis=-1, keepdims=True)
    ) / text_norm
    emb_grad_all = (
        unit_img_grad - unit_img * jnp.sum(unit_img * unit_img_grad, axis=-1, keepdims=True)
    ) / emb_norm
    text_grad = lax.dynamic_slice_in_dim(text_grad_all, first_row, batch_dev, axis=0)
    emb_grad = lax.dynamic_slice_in_dim(emb_grad_all, first_row, batch_dev, axis=0)
    weighted = dot_exact(emb_grad, proj, 1) * ln_gain
    weight_rows = weighted[:, None, None, :]
    weight_mean = jnp.mean(weighted, axis=-1)[:, None, None, None]
    spread_term = jnp.mean(weight_rows * normed, axis=-1, keepdims=True)
    grad_own = inv_dev * (weight_rows - weight_mean - normed * spread_term)
    grad_wide = with_halo(grad_own, (("space", 1),), reach_rows)
    grad_pad = jnp.pad(grad_wide, ((0, 0), (0, 0), (reach_rows, reach_rows), (0, 0)))
    blocks = channels // 128
    halves = ((0, blocks // 2), (blocks // 2, blocks - blocks // 2))
    input_parts = [
        [input_terms(grad_pad[image], kernel_float, row_count, *half) for image in range(batch_dev)]
        for half in halves
    ]
    kernel_part = kernel_terms(grad_own[0], padded_all[0], reach_rows)
    for image in range(1, batch_dev):
        kernel_part = kernel_part + kernel_terms(grad_own[image], padded_all[image], reach_rows)
    kernel_sum, input_parts = halving_sum(kernel_part, ("space", "dp"), 3, input_parts)
    input_grad = jnp.stack(
        [jnp.concatenate([half[image] for half in input_parts], axis=-1) for image in range(batch_dev)]
    )
    kernel_grad = kernel_sum / pixel_count
    return (loss, input_grad.astype(jnp.bfloat16), kernel_grad, text_grad)


def solution(mesh):
    placed = (P("dp", "space", None, None), P(), P(), P(), P(), P(), P("dp", None), P())
    return jax.shard_map(
        shards,
        mesh=mesh,
        in_specs=placed,
        out_specs=(P(), P("dp", "space", None, None), P(), P("dp", None)),
        check_vma=False,
    )
```

```python
import jax
import jax.numpy as jnp
from jax import lax
from jax.experimental import pallas as pl
from jax.sharding import PartitionSpec as P


def with_halo(block, sides, width):
    for axis, dim in sides:
        count = lax.axis_size(axis)
        forward = [(i, i + 1) for i in range(count - 1)]
        backward = [(target, source) for source, target in forward]
        low = lax.ppermute(
            lax.slice_in_dim(block, block.shape[dim] - width, None, axis=dim), axis, forward
        )
        high = lax.ppermute(lax.slice_in_dim(block, 0, width, axis=dim), axis, backward)
        block = jnp.concatenate([low, block, high], axis=dim)
    return block


def butterfly_sum(values, axes, riders=None):
    riders_done = None
    for axis in axes:
        count = lax.axis_size(axis)
        if count & (count - 1):
            values = lax.psum(values, axis)
            continue
        step = 1
        while step < count:
            pairs = [(i, i ^ step) for i in range(count)]
            received = lax.ppermute(values, axis, pairs)
            if riders is not None:
                received, riders = lax.optimization_barrier((received, riders))
                riders_done = riders
                riders = None
            values = values + received
            step *= 2
    return values if riders_done is None else (values, riders_done)


def halving_sum(values, axes, split_steps, riders):
    steps = []
    for axis in axes:
        count = lax.axis_size(axis)
        if count & (count - 1):
            return butterfly_sum(values, axes)
        step = 1
        while step < count:
            steps.append((axis, count, step))
            step *= 2
    split_steps = min(split_steps, len(steps))
    riders_done = []
    parts = 1 << split_steps
    flat = values.reshape(-1)
    size = flat.shape[0]
    padded_size = -(-size // parts) * parts
    chunk = jnp.pad(flat, (0, padded_size - size))
    for axis, count, step in steps[:split_steps]:
        pairs = [(i, i ^ step) for i in range(count)]
        upper = (lax.axis_index(axis) // step) % 2 == 1
        half = chunk.shape[0] // 2
        low, high = chunk[:half], chunk[half:]
        keep = jnp.where(upper, high, low)
        give = jnp.where(upper, low, high)
        received = lax.ppermute(give, axis, pairs)
        if len(riders_done) < len(riders):
            received, rider = lax.optimization_barrier((received, riders[len(riders_done)]))
            riders_done.append(rider)
        chunk = keep + received
    for axis, count, step in steps[split_steps:]:
        pairs = [(i, i ^ step) for i in range(count)]
        chunk = chunk + lax.ppermute(chunk, axis, pairs)
    for axis, count, step in reversed(steps[:split_steps]):
        pairs = [(i, i ^ step) for i in range(count)]
        upper = (lax.axis_index(axis) // step) % 2 == 1
        other = lax.ppermute(chunk, axis, pairs)
        chunk = jnp.where(
            upper, jnp.concatenate([other, chunk]), jnp.concatenate([chunk, other])
        )
    return chunk[:size].reshape(values.shape), riders_done


def normalize(values):
    centre_value = jnp.mean(values, axis=-1, keepdims=True)
    centred = values - centre_value
    spread = jnp.mean(centred * centred, axis=-1, keepdims=True)
    inv_dev = lax.rsqrt(spread + 1e-06)
    return (centred * inv_dev, inv_dev)


def depthwise(extended, kernel, reach_cols, **options):
    channels = kernel.shape[-1]
    return lax.conv_general_dilated(
        extended,
        kernel.reshape(kernel.shape[0], kernel.shape[1], 1, channels),
        (1, 1),
        ((0, 0), (reach_cols, reach_cols)),
        dimension_numbers=("NHWC", "HWIO", "NHWC"),
        feature_group_count=channels,
        **options,
    )


def kernel_terms(grad_rows, padded, reach, lanes=128):
    row_count, col_count, channels = grad_rows.shape
    side = 2 * reach + 1
    groups = col_count // 8

    def body(g_ref, x_ref, o_ref):
        for a in range(side):
            for d in range(side):
                acc = jnp.zeros((8, lanes), jnp.float32)
                for h in range(row_count):
                    prod = g_ref[h] * x_ref[h + a, pl.ds(d, col_count), :]
                    acc = acc + prod.reshape(groups, 8, lanes).sum(axis=0)
                o_ref[a, pl.ds(d, 1), :] = acc.sum(axis=0, keepdims=True)

    return pl.pallas_call(
        body,
        grid=(channels // lanes,),
        in_specs=[
            pl.BlockSpec((row_count, col_count, lanes), lambda i: (0, 0, i)),
            pl.BlockSpec(padded.shape[:2] + (lanes,), lambda i: (0, 0, i)),
        ],
        out_specs=pl.BlockSpec((side, side, lanes), lambda i: (0, 0, i)),
        out_shape=jax.ShapeDtypeStruct((side, side, channels), jnp.float32),
    )(grad_rows, padded)

def input_terms(padded, kernel, row_count, first_block, block_count, lanes=128):
    side = kernel.shape[0]
    col_count = padded.shape[1] - side + 1
    channels = padded.shape[2]

    def body(x_ref, k_ref, o_ref):
        for h in range(row_count):
            acc = jnp.zeros((col_count, lanes), jnp.float32)
            for a in range(side):
                for d in range(side):
                    weight = k_ref[side - 1 - a, pl.ds(side - 1 - d, 1), :]
                    acc = acc + weight * x_ref[h + a, pl.ds(d, col_count), :]
            o_ref[h] = acc.astype(o_ref.dtype)

    return pl.pallas_call(
        body,
        grid=(block_count,),
        in_specs=[
            pl.BlockSpec(padded.shape[:2] + (lanes,), lambda i: (0, 0, i + first_block)),
            pl.BlockSpec((side, side, lanes), lambda i: (0, 0, i + first_block)),
        ],
        out_specs=pl.BlockSpec((row_count, col_count, lanes), lambda i: (0, 0, i)),
        out_shape=jax.ShapeDtypeStruct((row_count, col_count, block_count * lanes), jnp.bfloat16),
    )(padded, kernel)

def logsum(scores, axis):
    highest = jnp.max(scores, axis=axis, keepdims=True)
    return jnp.squeeze(highest, axis) + jnp.log(jnp.sum(jnp.exp(scores - highest), axis=axis))


def shards(images, dw_kernel, dw_bias, ln_gain, ln_shift, proj, text, logit_scale):
    batch_dev, row_count, col_count, channels = images.shape
    height = row_count * lax.axis_size("space")
    pixel_count = height * col_count
    batch_count = batch_dev * lax.axis_size("dp")
    reach_rows = dw_kernel.shape[0] // 2
    kernel_float = dw_kernel.astype(jnp.float32)
    extended = with_halo(images, (("space", 1),), reach_rows)
    padded_all = jnp.pad(
        extended.astype(jnp.float32), ((0, 0), (0, 0), (reach_rows, reach_rows), (0, 0))
    )
    conv_out = (
        depthwise(extended, dw_kernel, reach_rows, preferred_element_type=jnp.float32) + dw_bias
    )
    normed, inv_dev = normalize(conv_out)
    pool_part = jnp.sum(normed * ln_gain + ln_shift, axis=(1, 2))
    pool_sum, padded_all = butterfly_sum(pool_part, ("space",), riders=padded_all)
    first_row = lax.axis_index("dp") * batch_dev
    packed = jnp.concatenate([pool_sum, text], axis=1)
    table = lax.dynamic_update_slice(
        jnp.zeros((batch_count, packed.shape[1]), jnp.float32), packed, (first_row, 0)
    )
    table = butterfly_sum(table, ("dp",))
    pooled = table[:, :channels] / pixel_count
    all_text = table[:, channels:]
    proj_float = proj.astype(jnp.float32)
    embedded = jnp.dot(pooled, proj_float, precision=lax.Precision.HIGHEST)
    emb_norm = jnp.sqrt(jnp.sum(embedded * embedded, axis=-1, keepdims=True))
    unit_img = embedded / emb_norm
    text_norm = jnp.sqrt(jnp.sum(all_text * all_text, axis=-1, keepdims=True))
    unit_txt = all_text / text_norm
    factor = logit_scale[0]
    scores = factor * jnp.dot(unit_img, unit_txt.T, precision=lax.Precision.HIGHEST)
    row_logsum = logsum(scores, 1)
    col_logsum = logsum(scores, 0)
    identity = jnp.eye(batch_count, dtype=jnp.float32)
    diagonal = jnp.sum(scores * identity, axis=1)
    loss = (jnp.sum(row_logsum - diagonal) + jnp.sum(col_logsum - diagonal)) / (2 * batch_count)
    score_grad = (
        0.5
        * (
            jnp.exp(scores - row_logsum[:, None])
            + jnp.exp(scores - col_logsum[None, :])
        )
        - identity
    )
    unit_img_grad = factor * jnp.dot(score_grad, unit_txt, precision=lax.Precision.HIGHEST)
    unit_txt_grad = factor * jnp.dot(score_grad.T, unit_img, precision=lax.Precision.HIGHEST)
    text_grad_all = (
        unit_txt_grad - unit_txt * jnp.sum(unit_txt * unit_txt_grad, axis=-1, keepdims=True)
    ) / text_norm
    emb_grad_all = (
        unit_img_grad - unit_img * jnp.sum(unit_img * unit_img_grad, axis=-1, keepdims=True)
    ) / emb_norm
    text_grad = lax.dynamic_slice_in_dim(text_grad_all, first_row, batch_dev, axis=0)
    emb_grad = lax.dynamic_slice_in_dim(emb_grad_all, first_row, batch_dev, axis=0)
    weighted = jnp.dot(emb_grad, proj_float.T, precision=lax.Precision.HIGHEST) * ln_gain
    weight_rows = weighted[:, None, None, :]
    weight_mean = jnp.mean(weighted, axis=-1)[:, None, None, None]
    spread_term = jnp.mean(weight_rows * normed, axis=-1, keepdims=True)
    grad_own = inv_dev * (weight_rows - weight_mean - normed * spread_term)
    grad_wide = with_halo(grad_own, (("space", 1),), reach_rows)
    grad_pad = jnp.pad(grad_wide, ((0, 0), (0, 0), (reach_rows, reach_rows), (0, 0)))
    blocks = channels // 128
    halves = ((0, blocks // 2), (blocks // 2, blocks - blocks // 2))
    input_parts = [
        [input_terms(grad_pad[image], kernel_float, row_count, *half) for image in range(batch_dev)]
        for half in halves
    ]
    kernel_part = kernel_terms(grad_own[0], padded_all[0], reach_rows)
    for image in range(1, batch_dev):
        kernel_part = kernel_part + kernel_terms(grad_own[image], padded_all[image], reach_rows)
    kernel_sum, input_parts = halving_sum(kernel_part, ("space", "dp"), 2, input_parts)
    input_grad = jnp.stack(
        [jnp.concatenate([half[image] for half in input_parts], axis=-1) for image in range(batch_dev)]
    )
    kernel_grad = kernel_sum / pixel_count
    return (loss, input_grad.astype(jnp.bfloat16), kernel_grad, text_grad)


def solution(mesh):
    placed = (P("dp", "space", None, None), P(), P(), P(), P(), P(), P("dp", None), P())
    return jax.shard_map(
        shards,
        mesh=mesh,
        in_specs=placed,
        out_specs=(P(), P("dp", "space", None, None), P(), P("dp", None)),
        check_vma=False,
    )
```

```python
import jax
import jax.numpy as jnp
from jax import lax
from jax.experimental import pallas as pl
from jax.sharding import PartitionSpec as P


def with_halo(block, sides, width):
    for axis, dim in sides:
        count = lax.axis_size(axis)
        forward = [(i, i + 1) for i in range(count - 1)]
        backward = [(target, source) for source, target in forward]
        low = lax.ppermute(
            lax.slice_in_dim(block, block.shape[dim] - width, None, axis=dim), axis, forward
        )
        high = lax.ppermute(lax.slice_in_dim(block, 0, width, axis=dim), axis, backward)
        block = jnp.concatenate([low, block, high], axis=dim)
    return block


def butterfly_sum(values, axes, riders=None):
    riders_done = None
    for axis in axes:
        count = lax.axis_size(axis)
        if count & (count - 1):
            values = lax.psum(values, axis)
            continue
        step = 1
        while step < count:
            pairs = [(i, i ^ step) for i in range(count)]
            received = lax.ppermute(values, axis, pairs)
            if riders is not None:
                received, riders = lax.optimization_barrier((received, riders))
                riders_done = riders
                riders = None
            values = values + received
            step *= 2
    return values if riders_done is None else (values, riders_done)


def halving_sum(values, axes, split_steps, riders):
    steps = []
    for axis in axes:
        count = lax.axis_size(axis)
        if count & (count - 1):
            return butterfly_sum(values, axes)
        step = 1
        while step < count:
            steps.append((axis, count, step))
            step *= 2
    nearest = [s for s in steps if s[2] == 1][1:]
    steps = steps[:2] + nearest + [s for s in steps[2:] if s not in nearest]
    split_steps = min(split_steps, len(steps))
    riders_done = []
    parts = 1 << split_steps
    flat = values.reshape(-1)
    size = flat.shape[0]
    padded_size = -(-size // parts) * parts
    chunk = jnp.pad(flat, (0, padded_size - size))
    for axis, count, step in steps[:split_steps]:
        pairs = [(i, i ^ step) for i in range(count)]
        upper = (lax.axis_index(axis) // step) % 2 == 1
        half = chunk.shape[0] // 2
        low, high = chunk[:half], chunk[half:]
        keep = jnp.where(upper, high, low)
        give = jnp.where(upper, low, high)
        received = lax.ppermute(give, axis, pairs)
        if len(riders_done) < len(riders):
            received, rider = lax.optimization_barrier((received, riders[len(riders_done)]))
            riders_done.append(rider)
        chunk = keep + received
    for axis, count, step in steps[split_steps:]:
        pairs = [(i, i ^ step) for i in range(count)]
        chunk = chunk + lax.ppermute(chunk, axis, pairs)
    for axis, count, step in reversed(steps[:split_steps]):
        pairs = [(i, i ^ step) for i in range(count)]
        upper = (lax.axis_index(axis) // step) % 2 == 1
        other = lax.ppermute(chunk, axis, pairs)
        chunk = jnp.where(
            upper, jnp.concatenate([other, chunk]), jnp.concatenate([chunk, other])
        )
    return chunk[:size].reshape(values.shape), riders_done


def normalize(values):
    centre_value = jnp.mean(values, axis=-1, keepdims=True)
    centred = values - centre_value
    spread = jnp.mean(centred * centred, axis=-1, keepdims=True)
    inv_dev = lax.rsqrt(spread + 1e-06)
    return (centred * inv_dev, inv_dev)


def depthwise(extended, kernel, reach_cols, **options):
    channels = kernel.shape[-1]
    return lax.conv_general_dilated(
        extended,
        kernel.reshape(kernel.shape[0], kernel.shape[1], 1, channels),
        (1, 1),
        ((0, 0), (reach_cols, reach_cols)),
        dimension_numbers=("NHWC", "HWIO", "NHWC"),
        feature_group_count=channels,
        **options,
    )


def kernel_terms(grad_rows, padded, reach, lanes=128):
    row_count, col_count, channels = grad_rows.shape
    side = 2 * reach + 1
    groups = col_count // 8

    def body(g_ref, x_ref, o_ref):
        for a in range(side):
            for d in range(side):
                acc = jnp.zeros((8, lanes), jnp.float32)
                for h in range(row_count):
                    prod = g_ref[h] * x_ref[h + a, pl.ds(d, col_count), :]
                    acc = acc + prod.reshape(groups, 8, lanes).sum(axis=0)
                o_ref[a, pl.ds(d, 1), :] = acc.sum(axis=0, keepdims=True)

    return pl.pallas_call(
        body,
        grid=(channels // lanes,),
        in_specs=[
            pl.BlockSpec((row_count, col_count, lanes), lambda i: (0, 0, i)),
            pl.BlockSpec(padded.shape[:2] + (lanes,), lambda i: (0, 0, i)),
        ],
        out_specs=pl.BlockSpec((side, side, lanes), lambda i: (0, 0, i)),
        out_shape=jax.ShapeDtypeStruct((side, side, channels), jnp.float32),
    )(grad_rows, padded)

def input_terms(padded, kernel, row_count, first_block, block_count, lanes=128):
    side = kernel.shape[0]
    col_count = padded.shape[1] - side + 1
    channels = padded.shape[2]

    def body(x_ref, k_ref, o_ref):
        for h in range(row_count):
            acc = jnp.zeros((col_count, lanes), jnp.float32)
            for a in range(side):
                for d in range(side):
                    weight = k_ref[side - 1 - a, pl.ds(side - 1 - d, 1), :]
                    acc = acc + weight * x_ref[h + a, pl.ds(d, col_count), :]
            o_ref[h] = acc.astype(o_ref.dtype)

    return pl.pallas_call(
        body,
        grid=(block_count,),
        in_specs=[
            pl.BlockSpec(padded.shape[:2] + (lanes,), lambda i: (0, 0, i + first_block)),
            pl.BlockSpec((side, side, lanes), lambda i: (0, 0, i + first_block)),
        ],
        out_specs=pl.BlockSpec((row_count, col_count, lanes), lambda i: (0, 0, i)),
        out_shape=jax.ShapeDtypeStruct((row_count, col_count, block_count * lanes), jnp.bfloat16),
    )(padded, kernel)

def logsum(scores, axis):
    highest = jnp.max(scores, axis=axis, keepdims=True)
    return jnp.squeeze(highest, axis) + jnp.log(jnp.sum(jnp.exp(scores - highest), axis=axis))


def shards(images, dw_kernel, dw_bias, ln_gain, ln_shift, proj, text, logit_scale):
    batch_dev, row_count, col_count, channels = images.shape
    height = row_count * lax.axis_size("space")
    pixel_count = height * col_count
    batch_count = batch_dev * lax.axis_size("dp")
    reach_rows = dw_kernel.shape[0] // 2
    kernel_float = dw_kernel.astype(jnp.float32)
    extended = with_halo(images, (("space", 1),), reach_rows)
    padded_all = jnp.pad(
        extended.astype(jnp.float32), ((0, 0), (0, 0), (reach_rows, reach_rows), (0, 0))
    )
    conv_out = (
        depthwise(extended, dw_kernel, reach_rows, preferred_element_type=jnp.float32) + dw_bias
    )
    normed, inv_dev = normalize(conv_out)
    pool_part = jnp.sum(normed * ln_gain + ln_shift, axis=(1, 2))
    pool_sum, padded_all = butterfly_sum(pool_part, ("space",), riders=padded_all)
    first_row = lax.axis_index("dp") * batch_dev
    packed = jnp.concatenate([pool_sum, text], axis=1)
    table = lax.dynamic_update_slice(
        jnp.zeros((batch_count, packed.shape[1]), jnp.float32), packed, (first_row, 0)
    )
    table = butterfly_sum(table, ("dp",))
    pooled = table[:, :channels] / pixel_count
    all_text = table[:, channels:]
    proj_float = proj.astype(jnp.float32)
    embedded = jnp.dot(pooled, proj_float, precision=lax.Precision.HIGHEST)
    emb_norm = jnp.sqrt(jnp.sum(embedded * embedded, axis=-1, keepdims=True))
    unit_img = embedded / emb_norm
    text_norm = jnp.sqrt(jnp.sum(all_text * all_text, axis=-1, keepdims=True))
    unit_txt = all_text / text_norm
    factor = logit_scale[0]
    scores = factor * jnp.dot(unit_img, unit_txt.T, precision=lax.Precision.HIGHEST)
    row_logsum = logsum(scores, 1)
    col_logsum = logsum(scores, 0)
    identity = jnp.eye(batch_count, dtype=jnp.float32)
    diagonal = jnp.sum(scores * identity, axis=1)
    loss = (jnp.sum(row_logsum - diagonal) + jnp.sum(col_logsum - diagonal)) / (2 * batch_count)
    score_grad = (
        0.5
        * (
            jnp.exp(scores - row_logsum[:, None])
            + jnp.exp(scores - col_logsum[None, :])
        )
        - identity
    )
    unit_img_grad = factor * jnp.dot(score_grad, unit_txt, precision=lax.Precision.HIGHEST)
    unit_txt_grad = factor * jnp.dot(score_grad.T, unit_img, precision=lax.Precision.HIGHEST)
    text_grad_all = (
        unit_txt_grad - unit_txt * jnp.sum(unit_txt * unit_txt_grad, axis=-1, keepdims=True)
    ) / text_norm
    emb_grad_all = (
        unit_img_grad - unit_img * jnp.sum(unit_img * unit_img_grad, axis=-1, keepdims=True)
    ) / emb_norm
    text_grad = lax.dynamic_slice_in_dim(text_grad_all, first_row, batch_dev, axis=0)
    emb_grad = lax.dynamic_slice_in_dim(emb_grad_all, first_row, batch_dev, axis=0)
    weighted = jnp.dot(emb_grad, proj_float.T, precision=lax.Precision.HIGHEST) * ln_gain
    weight_rows = weighted[:, None, None, :]
    weight_mean = jnp.mean(weighted, axis=-1)[:, None, None, None]
    spread_term = jnp.mean(weight_rows * normed, axis=-1, keepdims=True)
    grad_own = inv_dev * (weight_rows - weight_mean - normed * spread_term)
    grad_wide = with_halo(grad_own, (("space", 1),), reach_rows)
    grad_pad = jnp.pad(grad_wide, ((0, 0), (0, 0), (reach_rows, reach_rows), (0, 0)))
    blocks = channels // 128
    halves = ((0, blocks // 2), (blocks // 2, blocks - blocks // 2))
    input_parts = [
        [input_terms(grad_pad[image], kernel_float, row_count, *half) for image in range(batch_dev)]
        for half in halves
    ]
    kernel_part = kernel_terms(grad_own[0], padded_all[0], reach_rows)
    for image in range(1, batch_dev):
        kernel_part = kernel_part + kernel_terms(grad_own[image], padded_all[image], reach_rows)
    kernel_sum, input_parts = halving_sum(kernel_part, ("space", "dp"), 3, input_parts)
    input_grad = jnp.stack(
        [jnp.concatenate([half[image] for half in input_parts], axis=-1) for image in range(batch_dev)]
    )
    kernel_grad = kernel_sum / pixel_count
    return (loss, input_grad.astype(jnp.bfloat16), kernel_grad, text_grad)


def solution(mesh):
    placed = (P("dp", "space", None, None), P(), P(), P(), P(), P(), P("dp", None), P())
    return jax.shard_map(
        shards,
        mesh=mesh,
        in_specs=placed,
        out_specs=(P(), P("dp", "space", None, None), P(), P("dp", None)),
        check_vma=False,
    )
```
